128 devices in a mesh: req: 32 (over z, x, core), head: 4 (over y).
Axes of the slice: x: 4, y: 4, z: 4, core: 2. Of those that a mesh axis runs over, the one named last changes fastest.
Arguments:
- query_new: bfloat16 [2048, 5120], P('req', 'head'), may hold values from -6 to 6
- key_new: bfloat16 [2048, 5120], P('req', 'head'), may hold values from -6 to 6
- value_new: bfloat16 [2048, 5120], P('req', 'head'), may hold values from -6 to 6
- key_pool: bfloat16 [113152, 5120], P('req', 'head'), may hold values from -368 to 368
- value_pool: bfloat16 [113152, 5120], P('req', 'head'), may hold values from -6 to 6
- lengths: int32 [2048], replicated, may hold values from 8 to 1024, as said below
- slot_request: int32 [2048], replicated, may hold values from 0 to 2047, as said below
- residual: bfloat16 [2048, 5120], P(None, 'req'), may hold values from -6 to 6
- out_proj: bfloat16 [5120, 5120], P('head', 'req'), may hold values from -0.15625 to 0.15625
- norm_gain: bfloat16 [5120], replicated, may hold values from 0.5 to 1.5
- gate_proj: bfloat16 [5120, 13824], P(None, ('req', 'head')), may hold values from -0.078125 to 0.078125
- up_proj: bfloat16 [5120, 13824], P(None, ('req', 'head')), may hold values from -0.078125 to 0.078125
- down_proj: bfloat16 [13824, 5120], P('req', 'head'), may hold values from -0.21875 to 0.21875
Outputs:
- attended: bfloat16 [2048, 5120], P('head', 'req')
- ffn_out: bfloat16 [2048, 5120], P('req', 'head')
The draws below stay inside these ranges and needn't reach their ends.
Inputs may be any that keep to these rules, and one draw needn't show every extreme that they name: `slot_request`: a permutation of the requests; the 8 requests with more than 24 cached tokens sit two to an owner, on 4 owners. `lengths`: exactly 8 requests have 1024 // 2 to 1024 cached tokens and one of them has 1024; every other request has 8 to 24.
All inputs are finite; a program needn't handle non-finite values.
Results may differ from the reference program's by a relative error of at most 0.017.
Values may be sent and summed in bfloat16 or wider, within the bound.
No kernel may reach another device: no remote copies, remote signals or barrier semaphores. Data moves between devices by JAX's collectives and lax.ppermute only.
A program may use at most 192 MiB of HBM per device.

```python
import math
import jax
import jax.numpy as jnp
from jax import lax

D = 5120
H = 40
HD = 128
FF = 13824
REQ_DEV = 64
LONG_MAX = 1024
SHORT_MAX = 24
NLONG = 8
REQS = 2048
POOL = 3536
POOL_ALL = 113152
N_REQ = 32


def placement_tables(key):
    mixed_key = jax.random.fold_in(key, 11)
    key_order, key_hosts, key_offsets, key_short, key_long = jax.random.split(mixed_key, 5)
    slot_order = jax.random.permutation(key_order, REQS).astype(jnp.int32)
    long_hosts = jax.random.permutation(key_hosts, N_REQ)[:NLONG // 2].astype(jnp.int32)
    offsets = jax.random.permutation(key_offsets, REQ_DEV)[:2].astype(jnp.int32)
    long_slots = (long_hosts[:, None] * REQ_DEV + offsets[None, :]).reshape(-1)
    long_req = jnp.take(slot_order, long_slots)
    short_len = jax.random.randint(key_short, (REQS,), SHORT_MAX // 3, SHORT_MAX + 1, dtype=jnp.int32)
    long_len = jax.random.randint(key_long, (NLONG,), LONG_MAX // 2, LONG_MAX + 1, dtype=jnp.int32)
    long_len = long_len.at[0].set(LONG_MAX)
    return (slot_order, short_len.at[long_req].set(long_len))


def draw_lengths(key, part):
    return placement_tables(key)[1]


def draw_slot_request(key, part):
    return placement_tables(key)[0]


def draw_key_pool(key, part):
    normal_part = jnp.clip(jax.random.normal(key, (POOL_ALL, H * HD), jnp.float32), -6.0, 6.0)
    return normal_part.astype(jnp.bfloat16)


def level_of(key, dims, pieces, smallest, top_value):
    def one(axis_at, blocks):
        draws = jax.random.uniform(jax.random.fold_in(jax.random.fold_in(key, 6), axis_at), (blocks,), jnp.float32, smallest / len(pieces), top_value / len(pieces))
        return jnp.repeat(jnp.exp(draws), dims[axis_at] // blocks).reshape((-1,) + (1,) * (len(dims) - axis_at - 1))

    factor_of = one(*pieces[0])
    for cut in pieces[1:]:
        factor_of = factor_of * one(*cut)
    return factor_of


def normal_values(stream_key, shape, deviation, most, pieces=(), kind=jnp.bfloat16):
    entries = deviation * jax.random.normal(stream_key, shape, jnp.float32)
    if pieces:
        entries = entries * level_of(stream_key, shape, pieces, -0.22, 0.18)
    return jnp.clip(entries, -most, most).astype(kind)


def setup_inputs(seed: int = 0) -> dict:
    arg_keys = jax.random.split(jax.random.key(seed), 14)
    query_new = normal_values(arg_keys[0], (REQS, H * HD), 1.0, 6.0, ((0, 32), (1, 4)))
    key_new = normal_values(arg_keys[1], (REQS, H * HD), 1.0, 6.0, ((0, 32), (1, 4)))
    value_new = normal_values(arg_keys[2], (REQS, H * HD), 1.0, 6.0, ((0, 32), (1, 4)))
    key_pool = draw_key_pool(jax.random.fold_in(arg_keys[13], 71), 0)
    value_pool = normal_values(arg_keys[4], (POOL_ALL, H * HD), 1.0, 6.0, ((0, 32), (1, 4)))
    lengths = draw_lengths(jax.random.fold_in(arg_keys[13], 71), 0)
    slot_request = draw_slot_request(jax.random.fold_in(arg_keys[13], 71), 0)
    residual = normal_values(arg_keys[7], (REQS, D), 1.0, 6.0, ((1, 32),))
    out_proj = normal_values(arg_keys[8], (H * HD, D), (H * HD // 4) ** -0.5, 0.15625, ((0, 4), (1, 32)))
    norm_gain = jnp.clip(1.0 + 0.1 * jax.random.normal(arg_keys[9], (D,), jnp.float32), 0.5, 1.5).astype(jnp.bfloat16)
    gate_proj = normal_values(arg_keys[10], (D, FF), D ** -0.5, 0.078125, ((1, 128),))
    up_proj = normal_values(arg_keys[11], (D, FF), D ** -0.5, 0.078125, ((1, 128),))
    down_proj = normal_values(arg_keys[12], (FF, D), (FF // 16) ** -0.5, 0.21875, ((0, 32), (1, 4)))
    return dict(query_new=query_new, key_new=key_new, value_new=value_new, key_pool=key_pool, value_pool=value_pool, lengths=lengths, slot_request=slot_request, residual=residual, out_proj=out_proj, norm_gain=norm_gain, gate_proj=gate_proj, up_proj=up_proj, down_proj=down_proj)


def rope_tables(positions):
    half_dim = HD // 2
    freq_steps = jnp.arange(half_dim, dtype=jnp.float32)
    inverse = jnp.exp(freq_steps * (-2.0 * math.log(10000.0) / HD))
    angles = positions.astype(jnp.float32)[:, None] * inverse[None, :]
    return (jnp.cos(angles), jnp.sin(angles))

def rotate_half(vectors, cosine, sine_table):
    half_dim = HD // 2
    first_half = vectors[..., :half_dim]
    second = vectors[..., half_dim:]
    cos_grid = cosine[:, None, :]
    sin_grid = sine_table[:, None, :]
    return jnp.concatenate([first_half * cos_grid - second * sin_grid, second * cos_grid + first_half * sin_grid], axis=-1)

def attend(query_rot, key_rot, value_new, pool_keys, pool_values, seg_lengths):
    score_scale = HD ** (-0.5)
    seg_ends = jnp.cumsum(seg_lengths)
    starts = seg_ends - seg_lengths
    places = jnp.arange(pool_keys.shape[0], dtype=jnp.int32)
    member = (places[None, :] >= starts[:, None]) & (places[None, :] < seg_ends[:, None])
    scores = jnp.einsum('rgd,pgd->grp', query_rot.astype(jnp.float32), pool_keys.astype(jnp.float32)) * score_scale
    own_score = lax.optimization_barrier(jnp.sum(query_rot.astype(jnp.float32) * key_rot.astype(jnp.float32), axis=-1)).T * score_scale
    masked = jnp.where(member[None], scores, -jnp.inf)
    row_top = jnp.maximum(lax.optimization_barrier(jnp.max(masked, axis=-1)), own_score)
    weights = jnp.where(member[None], jnp.exp(scores - row_top[:, :, None]), 0.0)
    own_weight = jnp.exp(own_score - row_top)
    row_total = lax.optimization_barrier(jnp.sum(weights, axis=-1)) + own_weight
    weights_bf = lax.optimization_barrier(weights.astype(jnp.bfloat16)).astype(jnp.float32)
    own_bf = lax.optimization_barrier(own_weight.astype(jnp.bfloat16)).astype(jnp.float32)
    summed = jnp.einsum('grp,pgd->rgd', weights_bf, pool_values.astype(jnp.float32))
    summed = summed + own_bf.T[:, :, None] * value_new.astype(jnp.float32)
    return (summed / row_total.T[:, :, None]).astype(jnp.bfloat16)

def reference(query_new, key_new, value_new, key_pool, value_pool, lengths, slot_request, residual, out_proj, norm_gain, gate_proj, up_proj, down_proj):
    slot_length = jnp.take(lengths, slot_request, axis=0)
    cosine, sine_table = rope_tables(slot_length)
    shaped = (REQS, H, HD)
    query_rot = rotate_half(query_new.astype(jnp.float32).reshape(shaped), cosine, sine_table).astype(jnp.bfloat16)
    key_rot = rotate_half(key_new.astype(jnp.float32).reshape(shaped), cosine, sine_table).astype(jnp.bfloat16)
    values_new = value_new.reshape(shaped)

    def per_owner(owner):
        first_slot = (owner * REQ_DEV).astype(jnp.int32)
        first_row = (owner * POOL).astype(jnp.int32)
        pool_keys = lax.dynamic_slice_in_dim(key_pool, first_row, POOL, 0).reshape(POOL, H, HD)
        pool_values = lax.dynamic_slice_in_dim(value_pool, first_row, POOL, 0).reshape(POOL, H, HD)
        return attend(lax.dynamic_slice_in_dim(query_rot, first_slot, REQ_DEV, 0), lax.dynamic_slice_in_dim(key_rot, first_slot, REQ_DEV, 0), lax.dynamic_slice_in_dim(values_new, first_slot, REQ_DEV, 0), pool_keys, pool_values, lax.dynamic_slice_in_dim(slot_length, first_slot, REQ_DEV, 0))
    attention = lax.map(per_owner, jnp.arange(N_REQ, dtype=jnp.int32)).reshape(REQS, H * HD)
    projected = jnp.dot(attention, out_proj, preferred_element_type=jnp.float32)
    attended = (jnp.take(residual, slot_request, axis=0).astype(jnp.float32) + projected).astype(jnp.bfloat16)
    widened = attended.astype(jnp.float32)
    inverse = lax.rsqrt(lax.optimization_barrier(jnp.mean(widened * widened, axis=-1, keepdims=True)) + 1e-05)
    scaled = (widened * inverse * norm_gain.astype(jnp.float32)[None, :]).astype(jnp.bfloat16)
    gate_pre = jnp.dot(scaled, gate_proj, preferred_element_type=jnp.float32)
    upward = jnp.dot(scaled, up_proj, preferred_element_type=jnp.float32)
    active = (jax.nn.silu(gate_pre) * upward).astype(jnp.bfloat16)
    ffn_out = jnp.dot(active, down_proj, preferred_element_type=jnp.float32).astype(jnp.bfloat16)
    return (attended, ffn_out)
```

```python
import math

import jax
import jax.numpy as jnp
from jax import lax
from jax.experimental import pallas as pl
from jax.experimental.pallas import tpu as pltpu
from jax.sharding import PartitionSpec as P

D = 5120
HD = 128
HEADS_PER_STEP = 2
R_PER_STEP = 8


def rope_tables(positions):
    half_dim = HD // 2
    freq_steps = jnp.arange(half_dim, dtype=jnp.float32)
    inverse = jnp.exp(freq_steps * (-2.0 * math.log(10000.0) / HD))
    angles = positions.astype(jnp.float32)[:, None] * inverse[None, :]
    return (jnp.cos(angles), jnp.sin(angles))


def rotate_half(vectors, cosine, sine_table):
    half_dim = HD // 2
    first_half = vectors[..., :half_dim]
    second = vectors[..., half_dim:]
    cos_grid = cosine[:, None, :]
    sin_grid = sine_table[:, None, :]
    return jnp.concatenate(
        [first_half * cos_grid - second * sin_grid, second * cos_grid + first_half * sin_grid],
        axis=-1,
    )


def attention_kernel(start_ref, end_ref, q_ref, k_ref, vn_ref, kp_ref, vp_ref, o_ref):
    score_scale = HD ** (-0.5)
    slots = q_ref.shape[0]
    rows = kp_ref.shape[0]
    places = lax.broadcasted_iota(jnp.int32, (slots, rows), 1)
    member = (places >= start_ref[...]) & (places < end_ref[...])
    for j in range(HEADS_PER_STEP):
        cols = slice(j * HD, (j + 1) * HD)
        query = q_ref[:, cols]
        scores = (
            lax.dot_general(
                query,
                kp_ref[:, cols],
                (((1,), (1,)), ((), ())),
                preferred_element_type=jnp.float32,
            )
            * score_scale
        )
        own_score = (
            jnp.sum(
                query.astype(jnp.float32) * k_ref[:, cols].astype(jnp.float32),
                axis=-1,
                keepdims=True,
            )
            * score_scale
        )
        masked = jnp.where(member, scores, -jnp.inf)
        row_top = jnp.maximum(jnp.max(masked, axis=-1, keepdims=True), own_score)
        weights = jnp.where(member, jnp.exp(scores - row_top), 0.0)
        own_weight = jnp.exp(own_score - row_top)
        row_total = jnp.sum(weights, axis=-1, keepdims=True) + own_weight
        summed = jnp.dot(
            weights.astype(jnp.bfloat16), vp_ref[:, cols], preferred_element_type=jnp.float32
        )
        own_bf = own_weight.astype(jnp.bfloat16).astype(jnp.float32)
        summed = summed + own_bf * vn_ref[:, cols].astype(jnp.float32)
        o_ref[:, cols] = (summed / row_total).astype(o_ref.dtype)


def attend_local(query_rot, key_rot, value_new, key_pool, value_pool, starts, ends):
    slots, width = query_rot.shape
    rows = key_pool.shape[0]
    block = HEADS_PER_STEP * HD
    steps = width // block
    slot_spec = pl.BlockSpec((slots, block), lambda g: (0, g))
    pool_spec = pl.BlockSpec((rows, block), lambda g: (0, g))
    bound_spec = pl.BlockSpec((slots, 1), lambda g: (0, 0))
    flops = 4 * slots * rows * width
    return pl.pallas_call(
        attention_kernel,
        grid=(steps,),
        in_specs=[bound_spec, bound_spec, slot_spec, slot_spec, slot_spec, pool_spec, pool_spec],
        out_specs=slot_spec,
        out_shape=jax.ShapeDtypeStruct((slots, width), jnp.bfloat16),
        cost_estimate=pl.CostEstimate(
            flops=flops,
            transcendentals=slots * rows * (width // HD),
            bytes_accessed=2 * rows * width * 2 + 4 * slots * width * 2,
        ),
    )(starts, ends, query_rot, key_rot, value_new, key_pool, value_pool)


def gate_up_kernel(x_ref, wg_ref, wu_ref, o_ref, acc_gate, acc_up):
    step = pl.program_id(0)
    quarters = x_ref.shape[1]
    width = x_ref.shape[3]

    @pl.when(step == 0)
    def _():
        acc_gate[...] = jnp.zeros_like(acc_gate)
        acc_up[...] = jnp.zeros_like(acc_up)

    def body(i, carry):
        w_gate = wg_ref[i]
        w_up = wu_ref[i]
        for quarter in range(quarters):
            cols = slice(quarter * width, (quarter + 1) * width)
            block = x_ref[i, quarter]
            acc_gate[:, cols] += jnp.dot(w_gate, block, preferred_element_type=jnp.float32)
            acc_up[:, cols] += jnp.dot(w_up, block, preferred_element_type=jnp.float32)
        return carry

    lax.fori_loop(0, x_ref.shape[0], body, 0)

    @pl.when(step == pl.num_programs(0) - 1)
    def _():
        gate_pre = acc_gate[...]
        silu = gate_pre / (1.0 + jnp.exp(-gate_pre))
        o_ref[...] = (silu * acc_up[...]).astype(o_ref.dtype)


def gate_up(hidden_t, gate_t, up_t):
    chunks, quarters, columns, width = hidden_t.shape
    units = gate_t.shape[1]
    slots = quarters * width
    return pl.pallas_call(
        gate_up_kernel,
        grid=(chunks // R_PER_STEP,),
        in_specs=[
            pl.BlockSpec((R_PER_STEP, quarters, columns, width), lambda s: (s, 0, 0, 0)),
            pl.BlockSpec((R_PER_STEP, units, columns), lambda s: (s, 0, 0)),
            pl.BlockSpec((R_PER_STEP, units, columns), lambda s: (s, 0, 0)),
        ],
        out_specs=pl.BlockSpec((units, slots), lambda s: (0, 0)),
        out_shape=jax.ShapeDtypeStruct((units, slots), jnp.bfloat16),
        scratch_shapes=[
            pltpu.VMEM((units, slots), jnp.float32),
            pltpu.VMEM((units, slots), jnp.float32),
        ],
        compiler_params=pltpu.CompilerParams(dimension_semantics=("arbitrary",)),
        cost_estimate=pl.CostEstimate(
            flops=4 * units * slots * chunks * columns,
            transcendentals=units * slots,
            bytes_accessed=hidden_t.size * 2 + 2 * gate_t.size * 2 + units * slots * 2,
        ),
    )(hidden_t, gate_t, up_t)


def body(
    query_new,
    key_new,
    value_new,
    key_pool,
    value_pool,
    lengths,
    slot_request,
    residual,
    out_proj,
    norm_gain,
    gate_proj,
    up_proj,
    down_proj,
):
    owned = query_new.shape[0]
    groups = query_new.shape[1] // HD
    req_count = lax.axis_size("req")
    head_count = lax.axis_size("head")
    first_slot = lax.axis_index("req") * owned
    my_requests = lax.dynamic_slice_in_dim(slot_request, first_slot, owned, 0)
    my_lengths = jnp.take(lengths, my_requests, axis=0)
    cosine, sine_table = rope_tables(my_lengths)
    shaped = (owned, groups, HD)
    query_rot = rotate_half(
        query_new.astype(jnp.float32).reshape(shaped), cosine, sine_table
    ).astype(jnp.bfloat16)
    key_rot = rotate_half(key_new.astype(jnp.float32).reshape(shaped), cosine, sine_table).astype(
        jnp.bfloat16
    )
    seg_ends = jnp.cumsum(my_lengths)
    starts = (seg_ends - my_lengths).astype(jnp.int32)
    attention = attend_local(
        query_rot.reshape(owned, groups * HD),
        key_rot.reshape(owned, groups * HD),
        value_new,
        key_pool,
        value_pool,
        starts[:, None],
        seg_ends.astype(jnp.int32)[:, None],
    )
    partial_sums = jnp.dot(
        lax.all_gather(attention, "req", axis=0, tiled=True),
        out_proj,
        preferred_element_type=jnp.float32,
    )
    summed = lax.psum_scatter(partial_sums, "head", scatter_dimension=0, tiled=True)
    quarter = summed.shape[0]
    quarter_slots = lax.dynamic_slice_in_dim(
        slot_request, lax.axis_index("head") * quarter, quarter, 0
    )
    attended = (jnp.take(residual, quarter_slots, axis=0).astype(jnp.float32) + summed).astype(
        jnp.bfloat16
    )
    column_width = attended.shape[1]
    widened = attended.astype(jnp.float32)
    squares = lax.psum(jnp.sum(widened * widened, axis=1), "req")
    inverse = lax.rsqrt(squares / D + 1e-05)
    gain = lax.dynamic_slice_in_dim(
        norm_gain, lax.axis_index("req") * column_width, column_width, 0
    ).astype(jnp.float32)
    scaled = (widened * inverse[:, None] * gain[None, :]).astype(jnp.bfloat16)
    hidden_t = lax.all_gather(scaled.T[None], ("req", "head"), axis=0, tiled=True).reshape(
        req_count, head_count, column_width, quarter
    )
    col_block = gate_proj.shape[1]
    gate_t = gate_proj.reshape(req_count, column_width, col_block).transpose(0, 2, 1)
    up_t = up_proj.reshape(req_count, column_width, col_block).transpose(0, 2, 1)
    active_t = gate_up(hidden_t, gate_t, up_t)
    active_all = lax.all_gather(active_t, "head", axis=0, tiled=True)
    down_sums = lax.dot_general(
        active_all, down_proj, (((0,), (0,)), ((), ())), preferred_element_type=jnp.float32
    )
    ffn_out = lax.psum_scatter(
        down_sums.astype(jnp.bfloat16), "req", scatter_dimension=0, tiled=True
    )
    return (attended, ffn_out)


def solution(mesh):
    placed = (
        P("req", "head"),
        P("req", "head"),
        P("req", "head"),
        P("req", "head"),
        P("req", "head"),
        P(),
        P(),
        P(None, "req"),
        P("head", "req"),
        P(),
        P(None, ("req", "head")),
        P(None, ("req", "head")),
        P("req", "head"),
    )
    return jax.shard_map(
        body,
        mesh=mesh,
        in_specs=placed,
        out_specs=(P("head", "req"), P("req", "head")),
        check_vma=False,
    )
```

```python
import math

import jax
import jax.numpy as jnp
from jax import lax
from jax.experimental import pallas as pl
from jax.experimental.pallas import tpu as pltpu
from jax.sharding import PartitionSpec as P

D = 5120
HD = 128
HEADS_PER_STEP = 2
R_PER_STEP = 8


def rope_tables(positions):
    half_dim = HD // 2
    freq_steps = jnp.arange(half_dim, dtype=jnp.float32)
    inverse = jnp.exp(freq_steps * (-2.0 * math.log(10000.0) / HD))
    angles = positions.astype(jnp.float32)[:, None] * inverse[None, :]
    return (jnp.cos(angles), jnp.sin(angles))


def rotate_half(vectors, cosine, sine_table):
    half_dim = HD // 2
    first_half = vectors[..., :half_dim]
    second = vectors[..., half_dim:]
    cos_grid = cosine[:, None, :]
    sin_grid = sine_table[:, None, :]
    return jnp.concatenate(
        [first_half * cos_grid - second * sin_grid, second * cos_grid + first_half * sin_grid],
        axis=-1,
    )


def attention_kernel(start_ref, end_ref, q_ref, k_ref, vn_ref, kp_ref, vp_ref, o_ref):
    score_scale = HD ** (-0.5)
    slots = q_ref.shape[0]
    rows = kp_ref.shape[0]
    places = lax.broadcasted_iota(jnp.int32, (slots, rows), 1)
    member = (places >= start_ref[...]) & (places < end_ref[...])
    for j in range(HEADS_PER_STEP):
        cols = slice(j * HD, (j + 1) * HD)
        query = q_ref[:, cols]
        scores = (
            lax.dot_general(
                query,
                kp_ref[:, cols],
                (((1,), (1,)), ((), ())),
                preferred_element_type=jnp.float32,
            )
            * score_scale
        )
        own_score = (
            jnp.sum(
                query.astype(jnp.float32) * k_ref[:, cols].astype(jnp.float32),
                axis=-1,
                keepdims=True,
            )
            * score_scale
        )
        masked = jnp.where(member, scores, -jnp.inf)
        row_top = jnp.maximum(jnp.max(masked, axis=-1, keepdims=True), own_score)
        weights = jnp.where(member, jnp.exp(scores - row_top), 0.0)
        own_weight = jnp.exp(own_score - row_top)
        row_total = jnp.sum(weights, axis=-1, keepdims=True) + own_weight
        summed = jnp.dot(
            weights.astype(jnp.bfloat16), vp_ref[:, cols], preferred_element_type=jnp.float32
        )
        own_bf = own_weight.astype(jnp.bfloat16).astype(jnp.float32)
        summed = summed + own_bf * vn_ref[:, cols].astype(jnp.float32)
        o_ref[:, cols] = (summed / row_total).astype(o_ref.dtype)


def attend_local(query_rot, key_rot, value_new, key_pool, value_pool, starts, ends):
    slots, width = query_rot.shape
    rows = key_pool.shape[0]
    block = HEADS_PER_STEP * HD
    steps = width // block
    slot_spec = pl.BlockSpec((slots, block), lambda g: (0, g))
    pool_spec = pl.BlockSpec((rows, block), lambda g: (0, g))
    bound_spec = pl.BlockSpec((slots, 1), lambda g: (0, 0))
    flops = 4 * slots * rows * width
    return pl.pallas_call(
        attention_kernel,
        grid=(steps,),
        in_specs=[bound_spec, bound_spec, slot_spec, slot_spec, slot_spec, pool_spec, pool_spec],
        out_specs=slot_spec,
        out_shape=jax.ShapeDtypeStruct((slots, width), jnp.bfloat16),
        cost_estimate=pl.CostEstimate(
            flops=flops,
            transcendentals=slots * rows * (width // HD),
            bytes_accessed=2 * rows * width * 2 + 4 * slots * width * 2,
        ),
    )(starts, ends, query_rot, key_rot, value_new, key_pool, value_pool)


def gate_up_kernel(x_ref, wg_ref, wu_ref, o_ref, acc_gate, acc_up):
    step = pl.program_id(0)
    quarters = x_ref.shape[1]
    width = x_ref.shape[3]

    @pl.when(step == 0)
    def _():
        acc_gate[...] = jnp.zeros_like(acc_gate)
        acc_up[...] = jnp.zeros_like(acc_up)

    def body(i, carry):
        w_gate = wg_ref[i]
        w_up = wu_ref[i]
        for quarter in range(quarters):
            cols = slice(quarter * width, (quarter + 1) * width)
            block = x_ref[i, quarter]
            acc_gate[:, cols] += jnp.dot(w_gate, block, preferred_element_type=jnp.float32)
            acc_up[:, cols] += jnp.dot(w_up, block, preferred_element_type=jnp.float32)
        return carry

    lax.fori_loop(0, x_ref.shape[0], body, 0)

    @pl.when(step == pl.num_programs(0) - 1)
    def _():
        gate_pre = acc_gate[...]
        silu = gate_pre / (1.0 + jnp.exp(-gate_pre))
        o_ref[...] = (silu * acc_up[...]).astype(o_ref.dtype)


def gate_up(hidden_t, gate_t, up_t):
    chunks, quarters, columns, width = hidden_t.shape
    units = gate_t.shape[1]
    slots = quarters * width
    return pl.pallas_call(
        gate_up_kernel,
        grid=(chunks // R_PER_STEP,),
        in_specs=[
            pl.BlockSpec((R_PER_STEP, quarters, columns, width), lambda s: (s, 0, 0, 0)),
            pl.BlockSpec((R_PER_STEP, units, columns), lambda s: (s, 0, 0)),
            pl.BlockSpec((R_PER_STEP, units, columns), lambda s: (s, 0, 0)),
        ],
        out_specs=pl.BlockSpec((units, slots), lambda s: (0, 0)),
        out_shape=jax.ShapeDtypeStruct((units, slots), jnp.bfloat16),
        scratch_shapes=[
            pltpu.VMEM((units, slots), jnp.float32),
            pltpu.VMEM((units, slots), jnp.float32),
        ],
        compiler_params=pltpu.CompilerParams(dimension_semantics=("arbitrary",)),
        cost_estimate=pl.CostEstimate(
            flops=4 * units * slots * chunks * columns,
            transcendentals=units * slots,
            bytes_accessed=hidden_t.size * 2 + 2 * gate_t.size * 2 + units * slots * 2,
        ),
    )(hidden_t, gate_t, up_t)


def body(
    query_new,
    key_new,
    value_new,
    key_pool,
    value_pool,
    lengths,
    slot_request,
    residual,
    out_proj,
    norm_gain,
    gate_proj,
    up_proj,
    down_proj,
):
    owned = query_new.shape[0]
    groups = query_new.shape[1] // HD
    req_count = lax.axis_size("req")
    head_count = lax.axis_size("head")
    first_slot = lax.axis_index("req") * owned
    my_requests = lax.dynamic_slice_in_dim(slot_request, first_slot, owned, 0)
    my_lengths = jnp.take(lengths, my_requests, axis=0)
    cosine, sine_table = rope_tables(my_lengths)
    shaped = (owned, groups, HD)
    query_rot = rotate_half(
        query_new.astype(jnp.float32).reshape(shaped), cosine, sine_table
    ).astype(jnp.bfloat16)
    key_rot = rotate_half(key_new.astype(jnp.float32).reshape(shaped), cosine, sine_table).astype(
        jnp.bfloat16
    )
    seg_ends = jnp.cumsum(my_lengths)
    starts = (seg_ends - my_lengths).astype(jnp.int32)
    attention = attend_local(
        query_rot.reshape(owned, groups * HD),
        key_rot.reshape(owned, groups * HD),
        value_new,
        key_pool,
        value_pool,
        starts[:, None],
        seg_ends.astype(jnp.int32)[:, None],
    )
    partial_sums = jnp.dot(
        lax.all_gather(attention, "req", axis=0, tiled=True),
        out_proj,
        preferred_element_type=jnp.float32,
    )
    summed = lax.psum_scatter(partial_sums, "head", scatter_dimension=0, tiled=True)
    quarter = summed.shape[0]
    quarter_slots = lax.dynamic_slice_in_dim(
        slot_request, lax.axis_index("head") * quarter, quarter, 0
    )
    attended = (jnp.take(residual, quarter_slots, axis=0).astype(jnp.float32) + summed).astype(
        jnp.bfloat16
    )
    column_width = attended.shape[1]
    widened = attended.astype(jnp.float32)
    squares = jnp.sum(
        lax.all_gather(jnp.sum(widened * widened, axis=1), "req", axis=0), axis=0
    )
    inverse = lax.rsqrt(squares / D + 1e-05)
    gain = lax.dynamic_slice_in_dim(
        norm_gain, lax.axis_index("req") * column_width, column_width, 0
    ).astype(jnp.float32)
    scaled = (widened * inverse[:, None] * gain[None, :]).astype(jnp.bfloat16)
    hidden_t = lax.all_gather(scaled.T[None], ("req", "head"), axis=0, tiled=True).reshape(
        req_count, head_count, column_width, quarter
    )
    col_block = gate_proj.shape[1]
    gate_t = gate_proj.reshape(req_count, column_width, col_block).transpose(0, 2, 1)
    up_t = up_proj.reshape(req_count, column_width, col_block).transpose(0, 2, 1)
    active_t = gate_up(hidden_t, gate_t, up_t)
    active_all = lax.all_gather(active_t, "head", axis=0, tiled=True)
    down_sums = lax.dot_general(
        active_all, down_proj, (((0,), (0,)), ((), ())), preferred_element_type=jnp.float32
    )
    ffn_out = lax.psum_scatter(
        down_sums.astype(jnp.bfloat16), "req", scatter_dimension=0, tiled=True
    )
    return (attended, ffn_out)


def solution(mesh):
    placed = (
        P("req", "head"),
        P("req", "head"),
        P("req", "head"),
        P("req", "head"),
        P("req", "head"),
        P(),
        P(),
        P(None, "req"),
        P("head", "req"),
        P(),
        P(None, ("req", "head")),
        P(None, ("req", "head")),
        P("req", "head"),
    )
    return jax.shard_map(
        body,
        mesh=mesh,
        in_specs=placed,
        out_specs=(P("head", "req"), P("req", "head")),
        check_vma=False,
    )
```

```python
import math

import jax
import jax.numpy as jnp
from jax import lax
from jax.experimental import pallas as pl
from jax.experimental.pallas import tpu as pltpu
from jax.sharding import PartitionSpec as P

D = 5120
HD = 128
HEADS_PER_STEP = 2
R_PER_STEP = 8
SQ_ROWS = 16


def rope_tables(positions):
    half_dim = HD // 2
    freq_steps = jnp.arange(half_dim, dtype=jnp.float32)
    inverse = jnp.exp(freq_steps * (-2.0 * math.log(10000.0) / HD))
    angles = positions.astype(jnp.float32)[:, None] * inverse[None, :]
    return (jnp.cos(angles), jnp.sin(angles))


def rotate_half(vectors, cosine, sine_table):
    half_dim = HD // 2
    first_half = vectors[..., :half_dim]
    second = vectors[..., half_dim:]
    cos_grid = cosine[:, None, :]
    sin_grid = sine_table[:, None, :]
    return jnp.concatenate(
        [first_half * cos_grid - second * sin_grid, second * cos_grid + first_half * sin_grid],
        axis=-1,
    )


def attention_kernel(start_ref, end_ref, q_ref, k_ref, vn_ref, kp_ref, vp_ref, o_ref):
    score_scale = HD ** (-0.5)
    slots = q_ref.shape[0]
    rows = kp_ref.shape[0]
    places = lax.broadcasted_iota(jnp.int32, (slots, rows), 1)
    member = (places >= start_ref[...]) & (places < end_ref[...])
    for j in range(HEADS_PER_STEP):
        cols = slice(j * HD, (j + 1) * HD)
        query = q_ref[:, cols]
        scores = (
            lax.dot_general(
                query,
                kp_ref[:, cols],
                (((1,), (1,)), ((), ())),
                preferred_element_type=jnp.float32,
            )
            * score_scale
        )
        own_score = (
            jnp.sum(
                query.astype(jnp.float32) * k_ref[:, cols].astype(jnp.float32),
                axis=-1,
                keepdims=True,
            )
            * score_scale
        )
        masked = jnp.where(member, scores, -jnp.inf)
        row_top = jnp.maximum(jnp.max(masked, axis=-1, keepdims=True), own_score)
        weights = jnp.where(member, jnp.exp(scores - row_top), 0.0)
        own_weight = jnp.exp(own_score - row_top)
        row_total = jnp.sum(weights, axis=-1, keepdims=True) + own_weight
        summed = jnp.dot(
            weights.astype(jnp.bfloat16), vp_ref[:, cols], preferred_element_type=jnp.float32
        )
        own_bf = own_weight.astype(jnp.bfloat16).astype(jnp.float32)
        summed = summed + own_bf * vn_ref[:, cols].astype(jnp.float32)
        o_ref[:, cols] = (summed / row_total).astype(o_ref.dtype)


def attend_local(query_rot, key_rot, value_new, key_pool, value_pool, starts, ends):
    slots, width = query_rot.shape
    rows = key_pool.shape[0]
    block = HEADS_PER_STEP * HD
    steps = width // block
    slot_spec = pl.BlockSpec((slots, block), lambda g: (0, g))
    pool_spec = pl.BlockSpec((rows, block), lambda g: (0, g))
    bound_spec = pl.BlockSpec((slots, 1), lambda g: (0, 0))
    flops = 4 * slots * rows * width
    return pl.pallas_call(
        attention_kernel,
        grid=(steps,),
        in_specs=[bound_spec, bound_spec, slot_spec, slot_spec, slot_spec, pool_spec, pool_spec],
        out_specs=slot_spec,
        out_shape=jax.ShapeDtypeStruct((slots, width), jnp.bfloat16),
        cost_estimate=pl.CostEstimate(
            flops=flops,
            transcendentals=slots * rows * (width // HD),
            bytes_accessed=2 * rows * width * 2 + 4 * slots * width * 2,
        ),
    )(starts, ends, query_rot, key_rot, value_new, key_pool, value_pool)


def gate_up_kernel(x_ref, wg_ref, wu_ref, o_ref, acc_gate, acc_up, acc_sq):
    step = pl.program_id(0)
    quarters = x_ref.shape[1]
    width = x_ref.shape[3]
    columns = wg_ref.shape[2]

    @pl.when(step == 0)
    def _():
        acc_gate[...] = jnp.zeros_like(acc_gate)
        acc_up[...] = jnp.zeros_like(acc_up)
        acc_sq[...] = jnp.zeros_like(acc_sq)

    def body(i, carry):
        w_gate = wg_ref[i]
        w_up = wu_ref[i]
        for quarter in range(quarters):
            cols = slice(quarter * width, (quarter + 1) * width)
            block = x_ref[i, quarter, :columns, :]
            acc_gate[:, cols] += jnp.dot(w_gate, block, preferred_element_type=jnp.float32)
            acc_up[:, cols] += jnp.dot(w_up, block, preferred_element_type=jnp.float32)
            acc_sq[:, cols] += x_ref[i, quarter, columns:, :].astype(jnp.float32)
        return carry

    lax.fori_loop(0, x_ref.shape[0], body, 0)

    @pl.when(step == pl.num_programs(0) - 1)
    def _():
        squares = acc_sq[0:1, :] + acc_sq[1:2, :]
        inverse = lax.rsqrt(squares / D + 1e-05)
        gate_pre = acc_gate[...] * inverse
        silu = gate_pre / (1.0 + jnp.exp(-gate_pre))
        o_ref[...] = (silu * (acc_up[...] * inverse)).astype(o_ref.dtype)


def gate_up(hidden_t, gate_t, up_t):
    chunks, quarters, rows, width = hidden_t.shape
    units, columns = gate_t.shape[1], gate_t.shape[2]
    slots = quarters * width
    return pl.pallas_call(
        gate_up_kernel,
        grid=(chunks // R_PER_STEP,),
        in_specs=[
            pl.BlockSpec((R_PER_STEP, quarters, rows, width), lambda s: (s, 0, 0, 0)),
            pl.BlockSpec((R_PER_STEP, units, columns), lambda s: (s, 0, 0)),
            pl.BlockSpec((R_PER_STEP, units, columns), lambda s: (s, 0, 0)),
        ],
        out_specs=pl.BlockSpec((units, slots), lambda s: (0, 0)),
        out_shape=jax.ShapeDtypeStruct((units, slots), jnp.bfloat16),
        scratch_shapes=[
            pltpu.VMEM((units, slots), jnp.float32),
            pltpu.VMEM((units, slots), jnp.float32),
            pltpu.VMEM((rows - columns, slots), jnp.float32),
        ],
        compiler_params=pltpu.CompilerParams(dimension_semantics=("arbitrary",)),
        cost_estimate=pl.CostEstimate(
            flops=4 * units * slots * chunks * columns,
            transcendentals=units * slots,
            bytes_accessed=hidden_t.size * 2 + 2 * gate_t.size * 2 + units * slots * 2,
        ),
    )(hidden_t, gate_t, up_t)


def body(
    query_new,
    key_new,
    value_new,
    key_pool,
    value_pool,
    lengths,
    slot_request,
    residual,
    out_proj,
    norm_gain,
    gate_proj,
    up_proj,
    down_proj,
):
    owned = query_new.shape[0]
    groups = query_new.shape[1] // HD
    req_count = lax.axis_size("req")
    head_count = lax.axis_size("head")
    first_slot = lax.axis_index("req") * owned
    my_requests = lax.dynamic_slice_in_dim(slot_request, first_slot, owned, 0)
    my_lengths = jnp.take(lengths, my_requests, axis=0)
    cosine, sine_table = rope_tables(my_lengths)
    shaped = (owned, groups, HD)
    query_rot = rotate_half(
        query_new.astype(jnp.float32).reshape(shaped), cosine, sine_table
    ).astype(jnp.bfloat16)
    key_rot = rotate_half(key_new.astype(jnp.float32).reshape(shaped), cosine, sine_table).astype(
        jnp.bfloat16
    )
    seg_ends = jnp.cumsum(my_lengths)
    starts = (seg_ends - my_lengths).astype(jnp.int32)
    attention = attend_local(
        query_rot.reshape(owned, groups * HD),
        key_rot.reshape(owned, groups * HD),
        value_new,
        key_pool,
        value_pool,
        starts[:, None],
        seg_ends.astype(jnp.int32)[:, None],
    )
    partial_sums = jnp.dot(
        lax.all_gather(attention, "req", axis=0, tiled=True),
        out_proj,
        preferred_element_type=jnp.float32,
    )
    summed = lax.psum_scatter(partial_sums, "head", scatter_dimension=0, tiled=True)
    quarter = summed.shape[0]
    quarter_slots = lax.dynamic_slice_in_dim(
        slot_request, lax.axis_index("head") * quarter, quarter, 0
    )
    attended = (jnp.take(residual, quarter_slots, axis=0).astype(jnp.float32) + summed).astype(
        jnp.bfloat16
    )
    column_width = attended.shape[1]
    widened = attended.astype(jnp.float32)
    partial_squares = jnp.sum(widened * widened, axis=1)
    high = partial_squares.astype(jnp.bfloat16)
    low = (partial_squares - high.astype(jnp.float32)).astype(jnp.bfloat16)
    pad_rows = SQ_ROWS - 2
    block_t = jnp.concatenate(
        [attended.T, high[None], low[None], jnp.zeros((pad_rows, quarter), jnp.bfloat16)], axis=0
    )
    hidden_t = lax.all_gather(block_t[None], ("req", "head"), axis=0, tiled=True).reshape(
        req_count, head_count, column_width + SQ_ROWS, quarter
    )
    col_block = gate_proj.shape[1]
    gain = norm_gain.astype(jnp.float32)[:, None]
    gate_t = (
        (gate_proj.astype(jnp.float32) * gain)
        .astype(jnp.bfloat16)
        .reshape(req_count, column_width, col_block)
        .transpose(0, 2, 1)
    )
    up_t = (
        (up_proj.astype(jnp.float32) * gain)
        .astype(jnp.bfloat16)
        .reshape(req_count, column_width, col_block)
        .transpose(0, 2, 1)
    )
    active_t = gate_up(hidden_t, gate_t, up_t)
    active_all = lax.all_gather(active_t, "head", axis=0, tiled=True)
    down_sums = lax.dot_general(
        active_all, down_proj, (((0,), (0,)), ((), ())), preferred_element_type=jnp.float32
    )
    ffn_out = lax.psum_scatter(
        down_sums.astype(jnp.bfloat16), "req", scatter_dimension=0, tiled=True
    )
    return (attended, ffn_out)


def solution(mesh):
    placed = (
        P("req", "head"),
        P("req", "head"),
        P("req", "head"),
        P("req", "head"),
        P("req", "head"),
        P(),
        P(),
        P(None, "req"),
        P("head", "req"),
        P(),
        P(None, ("req", "head")),
        P(None, ("req", "head")),
        P("req", "head"),
    )
    return jax.shard_map(
        body,
        mesh=mesh,
        in_specs=placed,
        out_specs=(P("head", "req"), P("req", "head")),
        check_vma=False,
    )
```

```python
import math

import jax
import jax.numpy as jnp
from jax import lax
from jax.experimental import pallas as pl
from jax.experimental.pallas import tpu as pltpu
from jax.sharding import PartitionSpec as P

D = 5120
HD = 128
HEADS_PER_STEP = 2
R_PER_STEP = 8
SQ_ROWS = 16


def rope_tables(positions):
    half_dim = HD // 2
    freq_steps = jnp.arange(half_dim, dtype=jnp.float32)
    inverse = jnp.exp(freq_steps * (-2.0 * math.log(10000.0) / HD))
    angles = positions.astype(jnp.float32)[:, None] * inverse[None, :]
    return (jnp.cos(angles), jnp.sin(angles))


def rotate_half(vectors, cosine, sine_table):
    half_dim = HD // 2
    first_half = vectors[..., :half_dim]
    second = vectors[..., half_dim:]
    cos_grid = cosine[:, None, :]
    sin_grid = sine_table[:, None, :]
    return jnp.concatenate(
        [first_half * cos_grid - second * sin_grid, second * cos_grid + first_half * sin_grid],
        axis=-1,
    )


def attention_kernel(start_ref, end_ref, q_ref, k_ref, vn_ref, kp_ref, vp_ref, o_ref):
    score_scale = HD ** (-0.5)
    slots = q_ref.shape[0]
    rows = kp_ref.shape[0]
    places = lax.broadcasted_iota(jnp.int32, (slots, rows), 1)
    member = (places >= start_ref[...]) & (places < end_ref[...])
    for j in range(HEADS_PER_STEP):
        cols = slice(j * HD, (j + 1) * HD)
        query = q_ref[:, cols]
        scores = (
            lax.dot_general(
                query,
                kp_ref[:, cols],
                (((1,), (1,)), ((), ())),
                preferred_element_type=jnp.float32,
            )
            * score_scale
        )
        own_score = (
            jnp.sum(
                query.astype(jnp.float32) * k_ref[:, cols].astype(jnp.float32),
                axis=-1,
                keepdims=True,
            )
            * score_scale
        )
        masked = jnp.where(member, scores, -jnp.inf)
        row_top = jnp.maximum(jnp.max(masked, axis=-1, keepdims=True), own_score)
        weights = jnp.where(member, jnp.exp(scores - row_top), 0.0)
        own_weight = jnp.exp(own_score - row_top)
        row_total = jnp.sum(weights, axis=-1, keepdims=True) + own_weight
        summed = jnp.dot(
            weights.astype(jnp.bfloat16), vp_ref[:, cols], preferred_element_type=jnp.float32
        )
        own_bf = own_weight.astype(jnp.bfloat16).astype(jnp.float32)
        summed = summed + own_bf * vn_ref[:, cols].astype(jnp.float32)
        o_ref[:, cols] = (summed / row_total).astype(o_ref.dtype)


def attend_local(query_rot, key_rot, value_new, key_pool, value_pool, starts, ends):
    slots, width = query_rot.shape
    rows = key_pool.shape[0]
    block = HEADS_PER_STEP * HD
    steps = width // block
    slot_spec = pl.BlockSpec((slots, block), lambda g: (0, g))
    pool_spec = pl.BlockSpec((rows, block), lambda g: (0, g))
    bound_spec = pl.BlockSpec((slots, 1), lambda g: (0, 0))
    flops = 4 * slots * rows * width
    return pl.pallas_call(
        attention_kernel,
        grid=(steps,),
        in_specs=[bound_spec, bound_spec, slot_spec, slot_spec, slot_spec, pool_spec, pool_spec],
        out_specs=slot_spec,
        out_shape=jax.ShapeDtypeStruct((slots, width), jnp.bfloat16),
        cost_estimate=pl.CostEstimate(
            flops=flops,
            transcendentals=slots * rows * (width // HD),
            bytes_accessed=2 * rows * width * 2 + 4 * slots * width * 2,
        ),
    )(starts, ends, query_rot, key_rot, value_new, key_pool, value_pool)


def gate_up_kernel(x_ref, w_ref, o_ref, acc, acc_sq):
    step = pl.program_id(0)
    quarters = x_ref.shape[1]
    width = x_ref.shape[3]
    columns = w_ref.shape[2]
    half = w_ref.shape[1] // 2
    units = o_ref.shape[0]

    @pl.when(step == 0)
    def _():
        acc[...] = jnp.zeros_like(acc)
        acc_sq[...] = jnp.zeros_like(acc_sq)

    def body(i, carry):
        weights = w_ref[i]
        for quarter in range(quarters):
            cols = slice(quarter * width, (quarter + 1) * width)
            block = x_ref[i, quarter, :columns, :]
            acc[:, cols] += jnp.dot(weights, block, preferred_element_type=jnp.float32)
            acc_sq[:, cols] += x_ref[i, quarter, columns:, :].astype(jnp.float32)
        return carry

    lax.fori_loop(0, x_ref.shape[0], body, 0)

    @pl.when(step == pl.num_programs(0) - 1)
    def _():
        squares = acc_sq[0:1, :] + acc_sq[1:2, :]
        inverse = lax.rsqrt(squares / D + 1e-05)
        gate_pre = acc[:half, :] * inverse
        silu = gate_pre / (1.0 + jnp.exp(-gate_pre))
        active = silu * (acc[half:, :] * inverse)
        o_ref[...] = active[:units].astype(o_ref.dtype)


def gate_up(hidden_t, weights_t, units):
    chunks, quarters, rows, width = hidden_t.shape
    both, columns = weights_t.shape[1], weights_t.shape[2]
    slots = quarters * width
    return pl.pallas_call(
        gate_up_kernel,
        grid=(chunks // R_PER_STEP,),
        in_specs=[
            pl.BlockSpec((R_PER_STEP, quarters, rows, width), lambda s: (s, 0, 0, 0)),
            pl.BlockSpec((R_PER_STEP, both, columns), lambda s: (s, 0, 0)),
        ],
        out_specs=pl.BlockSpec((units, slots), lambda s: (0, 0)),
        out_shape=jax.ShapeDtypeStruct((units, slots), jnp.bfloat16),
        scratch_shapes=[
            pltpu.VMEM((both, slots), jnp.float32),
            pltpu.VMEM((rows - columns, slots), jnp.float32),
        ],
        compiler_params=pltpu.CompilerParams(dimension_semantics=("arbitrary",)),
        cost_estimate=pl.CostEstimate(
            flops=2 * both * slots * chunks * columns,
            transcendentals=units * slots,
            bytes_accessed=hidden_t.size * 2 + weights_t.size * 2 + units * slots * 2,
        ),
    )(hidden_t, weights_t)


def body(
    query_new,
    key_new,
    value_new,
    key_pool,
    value_pool,
    lengths,
    slot_request,
    residual,
    out_proj,
    norm_gain,
    gate_proj,
    up_proj,
    down_proj,
):
    owned = query_new.shape[0]
    groups = query_new.shape[1] // HD
    req_count = lax.axis_size("req")
    head_count = lax.axis_size("head")
    first_slot = lax.axis_index("req") * owned
    my_requests = lax.dynamic_slice_in_dim(slot_request, first_slot, owned, 0)
    my_lengths = jnp.take(lengths, my_requests, axis=0)
    cosine, sine_table = rope_tables(my_lengths)
    shaped = (owned, groups, HD)
    query_rot = rotate_half(
        query_new.astype(jnp.float32).reshape(shaped), cosine, sine_table
    ).astype(jnp.bfloat16)
    key_rot = rotate_half(key_new.astype(jnp.float32).reshape(shaped), cosine, sine_table).astype(
        jnp.bfloat16
    )
    seg_ends = jnp.cumsum(my_lengths)
    starts = (seg_ends - my_lengths).astype(jnp.int32)
    attention = attend_local(
        query_rot.reshape(owned, groups * HD),
        key_rot.reshape(owned, groups * HD),
        value_new,
        key_pool,
        value_pool,
        starts[:, None],
        seg_ends.astype(jnp.int32)[:, None],
    )
    partial_sums = jnp.dot(
        lax.all_gather(attention, "req", axis=0, tiled=True),
        out_proj,
        preferred_element_type=jnp.float32,
    )
    summed = lax.psum_scatter(partial_sums, "head", scatter_dimension=0, tiled=True)
    quarter = summed.shape[0]
    quarter_slots = lax.dynamic_slice_in_dim(
        slot_request, lax.axis_index("head") * quarter, quarter, 0
    )
    attended = (jnp.take(residual, quarter_slots, axis=0).astype(jnp.float32) + summed).astype(
        jnp.bfloat16
    )
    column_width = attended.shape[1]
    widened = attended.astype(jnp.float32)
    partial_squares = jnp.sum(widened * widened, axis=1)
    high = partial_squares.astype(jnp.bfloat16)
    low = (partial_squares - high.astype(jnp.float32)).astype(jnp.bfloat16)
    pad_rows = SQ_ROWS - 2
    block_t = jnp.concatenate(
        [attended.T, high[None], low[None], jnp.zeros((pad_rows, quarter), jnp.bfloat16)], axis=0
    )
    hidden_t = lax.all_gather(block_t[None], ("req", "head"), axis=0, tiled=True).reshape(
        req_count, head_count, column_width + SQ_ROWS, quarter
    )
    col_block = gate_proj.shape[1]
    gain = norm_gain.astype(jnp.float32)[:, None]
    padded = -(-col_block // 8) * 8

    def prepared(weights):
        scaled_w = (weights.astype(jnp.float32) * gain).astype(jnp.bfloat16)
        shaped_w = scaled_w.reshape(req_count, column_width, col_block).transpose(0, 2, 1)
        return jnp.pad(shaped_w, ((0, 0), (0, padded - col_block), (0, 0)))

    weights_t = jnp.concatenate([prepared(gate_proj), prepared(up_proj)], axis=1)
    active_t = gate_up(hidden_t, weights_t, col_block)
    active_all = lax.all_gather(active_t, "head", axis=0, tiled=True)
    down_sums = lax.dot_general(
        active_all, down_proj, (((0,), (0,)), ((), ())), preferred_element_type=jnp.float32
    )
    pieces = down_sums.astype(jnp.bfloat16).reshape(req_count, owned, down_sums.shape[1])
    received = lax.all_to_all(pieces, "req", 0, 0, tiled=True)
    ffn_out = jnp.sum(received.astype(jnp.float32), axis=0).astype(jnp.bfloat16)
    return (attended, ffn_out)


def solution(mesh):
    placed = (
        P("req", "head"),
        P("req", "head"),
        P("req", "head"),
        P("req", "head"),
        P("req", "head"),
        P(),
        P(),
        P(None, "req"),
        P("head", "req"),
        P(),
        P(None, ("req", "head")),
        P(None, ("req", "head")),
        P("req", "head"),
    )
    return jax.shard_map(
        body,
        mesh=mesh,
        in_specs=placed,
        out_specs=(P("head", "req"), P("req", "head")),
        check_vma=False,
    )
```

```python
import math

import jax
import jax.numpy as jnp
from jax import lax
from jax.experimental import pallas as pl
from jax.experimental.pallas import tpu as pltpu
from jax.sharding import PartitionSpec as P

D = 5120
HD = 128
HEADS_PER_STEP = 2
R_PER_STEP = 8
SQ_ROWS = 16
FFN_PARTS = 2


def rope_tables(positions):
    half_dim = HD // 2
    freq_steps = jnp.arange(half_dim, dtype=jnp.float32)
    inverse = jnp.exp(freq_steps * (-2.0 * math.log(10000.0) / HD))
    angles = positions.astype(jnp.float32)[:, None] * inverse[None, :]
    return (jnp.cos(angles), jnp.sin(angles))


def rotate_half(vectors, cosine, sine_table):
    half_dim = HD // 2
    first_half = vectors[..., :half_dim]
    second = vectors[..., half_dim:]
    cos_grid = cosine[:, None, :]
    sin_grid = sine_table[:, None, :]
    return jnp.concatenate(
        [first_half * cos_grid - second * sin_grid, second * cos_grid + first_half * sin_grid],
        axis=-1,
    )


def attention_kernel(start_ref, end_ref, q_ref, k_ref, vn_ref, kp_ref, vp_ref, o_ref):
    score_scale = HD ** (-0.5)
    slots = q_ref.shape[0]
    rows = kp_ref.shape[0]
    places = lax.broadcasted_iota(jnp.int32, (slots, rows), 1)
    member = (places >= start_ref[...]) & (places < end_ref[...])
    for j in range(HEADS_PER_STEP):
        cols = slice(j * HD, (j + 1) * HD)
        query = q_ref[:, cols]
        scores = (
            lax.dot_general(
                query,
                kp_ref[:, cols],
                (((1,), (1,)), ((), ())),
                preferred_element_type=jnp.float32,
            )
            * score_scale
        )
        own_score = (
            jnp.sum(
                query.astype(jnp.float32) * k_ref[:, cols].astype(jnp.float32),
                axis=-1,
                keepdims=True,
            )
            * score_scale
        )
        masked = jnp.where(member, scores, -jnp.inf)
        row_top = jnp.maximum(jnp.max(masked, axis=-1, keepdims=True), own_score)
        weights = jnp.where(member, jnp.exp(scores - row_top), 0.0)
        own_weight = jnp.exp(own_score - row_top)
        row_total = jnp.sum(weights, axis=-1, keepdims=True) + own_weight
        summed = jnp.dot(
            weights.astype(jnp.bfloat16), vp_ref[:, cols], preferred_element_type=jnp.float32
        )
        own_bf = own_weight.astype(jnp.bfloat16).astype(jnp.float32)
        summed = summed + own_bf * vn_ref[:, cols].astype(jnp.float32)
        o_ref[:, cols] = (summed / row_total).astype(o_ref.dtype)


def attend_local(query_rot, key_rot, value_new, key_pool, value_pool, starts, ends):
    slots, width = query_rot.shape
    rows = key_pool.shape[0]
    block = HEADS_PER_STEP * HD
    steps = width // block
    slot_spec = pl.BlockSpec((slots, block), lambda g: (0, g))
    pool_spec = pl.BlockSpec((rows, block), lambda g: (0, g))
    bound_spec = pl.BlockSpec((slots, 1), lambda g: (0, 0))
    flops = 4 * slots * rows * width
    return pl.pallas_call(
        attention_kernel,
        grid=(steps,),
        in_specs=[bound_spec, bound_spec, slot_spec, slot_spec, slot_spec, pool_spec, pool_spec],
        out_specs=slot_spec,
        out_shape=jax.ShapeDtypeStruct((slots, width), jnp.bfloat16),
        cost_estimate=pl.CostEstimate(
            flops=flops,
            transcendentals=slots * rows * (width // HD),
            bytes_accessed=2 * rows * width * 2 + 4 * slots * width * 2,
        ),
    )(starts, ends, query_rot, key_rot, value_new, key_pool, value_pool)


def gate_up_kernel(x_ref, w_ref, o_ref, acc, acc_sq):
    step = pl.program_id(0)
    quarters = x_ref.shape[1]
    width = x_ref.shape[3]
    columns = w_ref.shape[2]
    half = w_ref.shape[1] // 2
    units = o_ref.shape[0]

    @pl.when(step == 0)
    def _():
        acc[...] = jnp.zeros_like(acc)
        acc_sq[...] = jnp.zeros_like(acc_sq)

    def body(i, carry):
        weights = w_ref[i]
        for quarter in range(quarters):
            cols = slice(quarter * width, (quarter + 1) * width)
            block = x_ref[i, quarter, :columns, :]
            acc[:, cols] += jnp.dot(weights, block, preferred_element_type=jnp.float32)
            acc_sq[:, cols] += x_ref[i, quarter, columns:, :].astype(jnp.float32)
        return carry

    lax.fori_loop(0, x_ref.shape[0], body, 0)

    @pl.when(step == pl.num_programs(0) - 1)
    def _():
        squares = acc_sq[0:1, :] + acc_sq[1:2, :]
        inverse = lax.rsqrt(squares / D + 1e-05)
        gate_pre = acc[:half, :] * inverse
        silu = gate_pre / (1.0 + jnp.exp(-gate_pre))
        active = silu * (acc[half:, :] * inverse)
        o_ref[...] = active[:units].astype(o_ref.dtype)


def gate_up(hidden_t, weights_t, units):
    chunks, quarters, rows, width = hidden_t.shape
    both, columns = weights_t.shape[1], weights_t.shape[2]
    slots = quarters * width
    return pl.pallas_call(
        gate_up_kernel,
        grid=(chunks // R_PER_STEP,),
        in_specs=[
            pl.BlockSpec((R_PER_STEP, quarters, rows, width), lambda s: (s, 0, 0, 0)),
            pl.BlockSpec((R_PER_STEP, both, columns), lambda s: (s, 0, 0)),
        ],
        out_specs=pl.BlockSpec((units, slots), lambda s: (0, 0)),
        out_shape=jax.ShapeDtypeStruct((units, slots), jnp.bfloat16),
        scratch_shapes=[
            pltpu.VMEM((both, slots), jnp.float32),
            pltpu.VMEM((rows - columns, slots), jnp.float32),
        ],
        compiler_params=pltpu.CompilerParams(dimension_semantics=("arbitrary",)),
        cost_estimate=pl.CostEstimate(
            flops=2 * both * slots * chunks * columns,
            transcendentals=units * slots,
            bytes_accessed=hidden_t.size * 2 + weights_t.size * 2 + units * slots * 2,
        ),
    )(hidden_t, weights_t)


def body(
    query_new,
    key_new,
    value_new,
    key_pool,
    value_pool,
    lengths,
    slot_request,
    residual,
    out_proj,
    norm_gain,
    gate_proj,
    up_proj,
    down_proj,
):
    owned = query_new.shape[0]
    groups = query_new.shape[1] // HD
    req_count = lax.axis_size("req")
    head_count = lax.axis_size("head")
    first_slot = lax.axis_index("req") * owned
    my_requests = lax.dynamic_slice_in_dim(slot_request, first_slot, owned, 0)
    my_lengths = jnp.take(lengths, my_requests, axis=0)
    cosine, sine_table = rope_tables(my_lengths)
    shaped = (owned, groups, HD)
    query_rot = rotate_half(
        query_new.astype(jnp.float32).reshape(shaped), cosine, sine_table
    ).astype(jnp.bfloat16)
    key_rot = rotate_half(key_new.astype(jnp.float32).reshape(shaped), cosine, sine_table).astype(
        jnp.bfloat16
    )
    seg_ends = jnp.cumsum(my_lengths)
    starts = (seg_ends - my_lengths).astype(jnp.int32)
    attention = attend_local(
        query_rot.reshape(owned, groups * HD),
        key_rot.reshape(owned, groups * HD),
        value_new,
        key_pool,
        value_pool,
        starts[:, None],
        seg_ends.astype(jnp.int32)[:, None],
    )
    partial_sums = jnp.dot(
        lax.all_gather(attention, "req", axis=0, tiled=True),
        out_proj,
        preferred_element_type=jnp.float32,
    )
    summed = lax.psum_scatter(partial_sums, "head", scatter_dimension=0, tiled=True)
    quarter = summed.shape[0]
    quarter_slots = lax.dynamic_slice_in_dim(
        slot_request, lax.axis_index("head") * quarter, quarter, 0
    )
    attended = (jnp.take(residual, quarter_slots, axis=0).astype(jnp.float32) + summed).astype(
        jnp.bfloat16
    )
    column_width = attended.shape[1]
    widened = attended.astype(jnp.float32)
    partial_squares = jnp.sum(widened * widened, axis=1)
    high = partial_squares.astype(jnp.bfloat16)
    low = (partial_squares - high.astype(jnp.float32)).astype(jnp.bfloat16)
    pad_rows = SQ_ROWS - 2
    block_t = jnp.concatenate(
        [attended.T, high[None], low[None], jnp.zeros((pad_rows, quarter), jnp.bfloat16)], axis=0
    )
    col_block = gate_proj.shape[1]
    gain = norm_gain.astype(jnp.float32)[:, None]
    padded = -(-col_block // 8) * 8

    def prepared(weights):
        scaled_w = (weights.astype(jnp.float32) * gain).astype(jnp.bfloat16)
        shaped_w = scaled_w.reshape(req_count, column_width, col_block).transpose(0, 2, 1)
        return jnp.pad(shaped_w, ((0, 0), (0, padded - col_block), (0, 0)))

    weights_t = jnp.concatenate([prepared(gate_proj), prepared(up_proj)], axis=1)
    owners = quarter // owned
    split = owned // FFN_PARTS
    rows = block_t.shape[0]
    parts = block_t.reshape(rows, owners, FFN_PARTS, split)
    outputs = []
    for part in range(FFN_PARTS):
        piece = parts[:, :, part, :].reshape(rows, owners * split)
        hidden_t = lax.all_gather(piece[None], ("req", "head"), axis=0, tiled=True).reshape(
            req_count, head_count, rows, owners * split
        )
        active_t = gate_up(hidden_t, weights_t, col_block)
        active_all = lax.all_gather(active_t, "head", axis=0, tiled=True)
        down_sums = lax.dot_general(
            active_all, down_proj, (((0,), (0,)), ((), ())), preferred_element_type=jnp.float32
        )
        pieces = down_sums.astype(jnp.bfloat16).reshape(req_count, split, down_sums.shape[1])
        received = lax.all_to_all(pieces, "req", 0, 0, tiled=True)
        outputs.append(jnp.sum(received.astype(jnp.float32), axis=0))
    ffn_out = jnp.concatenate(outputs, axis=0).astype(jnp.bfloat16)
    return (attended, ffn_out)


def solution(mesh):
    placed = (
        P("req", "head"),
        P("req", "head"),
        P("req", "head"),
        P("req", "head"),
        P("req", "head"),
        P(),
        P(),
        P(None, "req"),
        P("head", "req"),
        P(),
        P(None, ("req", "head")),
        P(None, ("req", "head")),
        P("req", "head"),
    )
    return jax.shard_map(
        body,
        mesh=mesh,
        in_specs=placed,
        out_specs=(P("head", "req"), P("req", "head")),
        check_vma=False,
    )
```

```python
import math

import jax
import jax.numpy as jnp
from jax import lax
from jax.experimental import pallas as pl
from jax.experimental.pallas import tpu as pltpu
from jax.sharding import PartitionSpec as P

D = 5120
HD = 128
CHIPS = "chip"
CORE = "core"
REQ = (CHIPS, CORE)
CORES_PER_CHIP = 2
HEAD = "y"
HEADS_PER_STEP = 2
R_PER_STEP = 8
SQ_ROWS = 16


def rope_tables(positions):
    half_dim = HD // 2
    freq_steps = jnp.arange(half_dim, dtype=jnp.float32)
    inverse = jnp.exp(freq_steps * (-2.0 * math.log(10000.0) / HD))
    angles = positions.astype(jnp.float32)[:, None] * inverse[None, :]
    return (jnp.cos(angles), jnp.sin(angles))


def rotate_half(vectors, cosine, sine_table):
    half_dim = HD // 2
    first_half = vectors[..., :half_dim]
    second = vectors[..., half_dim:]
    cos_grid = cosine[:, None, :]
    sin_grid = sine_table[:, None, :]
    return jnp.concatenate(
        [first_half * cos_grid - second * sin_grid, second * cos_grid + first_half * sin_grid],
        axis=-1,
    )


def attention_kernel(start_ref, end_ref, q_ref, k_ref, vn_ref, kp_ref, vp_ref, o_ref):
    score_scale = HD ** (-0.5)
    slots = q_ref.shape[0]
    rows = kp_ref.shape[0]
    places = lax.broadcasted_iota(jnp.int32, (slots, rows), 1)
    member = (places >= start_ref[...]) & (places < end_ref[...])
    for j in range(HEADS_PER_STEP):
        cols = slice(j * HD, (j + 1) * HD)
        query = q_ref[:, cols]
        scores = (
            lax.dot_general(
                query,
                kp_ref[:, cols],
                (((1,), (1,)), ((), ())),
                preferred_element_type=jnp.float32,
            )
            * score_scale
        )
        own_score = (
            jnp.sum(
                query.astype(jnp.float32) * k_ref[:, cols].astype(jnp.float32),
                axis=-1,
                keepdims=True,
            )
            * score_scale
        )
        masked = jnp.where(member, scores, -jnp.inf)
        row_top = jnp.maximum(jnp.max(masked, axis=-1, keepdims=True), own_score)
        weights = jnp.where(member, jnp.exp(scores - row_top), 0.0)
        own_weight = jnp.exp(own_score - row_top)
        row_total = jnp.sum(weights, axis=-1, keepdims=True) + own_weight
        summed = jnp.dot(
            weights.astype(jnp.bfloat16), vp_ref[:, cols], preferred_element_type=jnp.float32
        )
        own_bf = own_weight.astype(jnp.bfloat16).astype(jnp.float32)
        summed = summed + own_bf * vn_ref[:, cols].astype(jnp.float32)
        o_ref[:, cols] = (summed / row_total).astype(o_ref.dtype)


def attend_local(query_rot, key_rot, value_new, key_pool, value_pool, starts, ends):
    slots, width = query_rot.shape
    rows = key_pool.shape[0]
    block = HEADS_PER_STEP * HD
    steps = width // block
    slot_spec = pl.BlockSpec((slots, block), lambda g: (0, g))
    pool_spec = pl.BlockSpec((rows, block), lambda g: (0, g))
    bound_spec = pl.BlockSpec((slots, 1), lambda g: (0, 0))
    flops = 4 * slots * rows * width
    return pl.pallas_call(
        attention_kernel,
        grid=(steps,),
        in_specs=[bound_spec, bound_spec, slot_spec, slot_spec, slot_spec, pool_spec, pool_spec],
        out_specs=slot_spec,
        out_shape=jax.ShapeDtypeStruct((slots, width), jnp.bfloat16),
        cost_estimate=pl.CostEstimate(
            flops=flops,
            transcendentals=slots * rows * (width // HD),
            bytes_accessed=2 * rows * width * 2 + 4 * slots * width * 2,
        ),
    )(starts, ends, query_rot, key_rot, value_new, key_pool, value_pool)


def gate_up_kernel(x_ref, w_ref, o_ref, acc, acc_sq):
    step = pl.program_id(0)
    quarters = x_ref.shape[1]
    width = x_ref.shape[3]
    columns = w_ref.shape[2]
    half = w_ref.shape[1] // 2
    units = o_ref.shape[0]

    @pl.when(step == 0)
    def _():
        acc[...] = jnp.zeros_like(acc)
        acc_sq[...] = jnp.zeros_like(acc_sq)

    def body(i, carry):
        weights = w_ref[i]
        for quarter in range(quarters):
            cols = slice(quarter * width, (quarter + 1) * width)
            block = x_ref[i, quarter, :columns, :]
            acc[:, cols] += jnp.dot(weights, block, preferred_element_type=jnp.float32)
            acc_sq[:, cols] += x_ref[i, quarter, columns:, :].astype(jnp.float32)
        return carry

    lax.fori_loop(0, x_ref.shape[0], body, 0)

    @pl.when(step == pl.num_programs(0) - 1)
    def _():
        squares = acc_sq[0:1, :] + acc_sq[1:2, :]
        inverse = lax.rsqrt(squares / D + 1e-05)
        gate_pre = acc[:half, :] * inverse
        silu = gate_pre / (1.0 + jnp.exp(-gate_pre))
        active = silu * (acc[half:, :] * inverse)
        o_ref[...] = active[:units].astype(o_ref.dtype)


def gate_up(hidden_t, weights_t, units):
    chunks, quarters, rows, width = hidden_t.shape
    both, columns = weights_t.shape[1], weights_t.shape[2]
    slots = quarters * width
    return pl.pallas_call(
        gate_up_kernel,
        grid=(chunks // R_PER_STEP,),
        in_specs=[
            pl.BlockSpec((R_PER_STEP, quarters, rows, width), lambda s: (s, 0, 0, 0)),
            pl.BlockSpec((R_PER_STEP, both, columns), lambda s: (s, 0, 0)),
        ],
        out_specs=pl.BlockSpec((units, slots), lambda s: (0, 0)),
        out_shape=jax.ShapeDtypeStruct((units, slots), jnp.bfloat16),
        scratch_shapes=[
            pltpu.VMEM((both, slots), jnp.float32),
            pltpu.VMEM((rows - columns, slots), jnp.float32),
        ],
        compiler_params=pltpu.CompilerParams(dimension_semantics=("arbitrary",)),
        cost_estimate=pl.CostEstimate(
            flops=2 * both * slots * chunks * columns,
            transcendentals=units * slots,
            bytes_accessed=hidden_t.size * 2 + weights_t.size * 2 + units * slots * 2,
        ),
    )(hidden_t, weights_t)


def body(
    query_new,
    key_new,
    value_new,
    key_pool,
    value_pool,
    lengths,
    slot_request,
    residual,
    out_proj,
    norm_gain,
    gate_proj,
    up_proj,
    down_proj,
):
    owned = query_new.shape[0]
    groups = query_new.shape[1] // HD
    req_count = lax.axis_size(REQ)
    head_count = lax.axis_size(HEAD)
    first_slot = lax.axis_index(REQ) * owned
    my_requests = lax.dynamic_slice_in_dim(slot_request, first_slot, owned, 0)
    my_lengths = jnp.take(lengths, my_requests, axis=0)
    cosine, sine_table = rope_tables(my_lengths)
    shaped = (owned, groups, HD)
    query_rot = rotate_half(
        query_new.astype(jnp.float32).reshape(shaped), cosine, sine_table
    ).astype(jnp.bfloat16)
    key_rot = rotate_half(key_new.astype(jnp.float32).reshape(shaped), cosine, sine_table).astype(
        jnp.bfloat16
    )
    seg_ends = jnp.cumsum(my_lengths)
    starts = (seg_ends - my_lengths).astype(jnp.int32)
    attention = attend_local(
        query_rot.reshape(owned, groups * HD),
        key_rot.reshape(owned, groups * HD),
        value_new,
        key_pool,
        value_pool,
        starts[:, None],
        seg_ends.astype(jnp.int32)[:, None],
    )
    partial_sums = jnp.dot(
        lax.all_gather(attention, REQ, axis=0, tiled=True),
        out_proj,
        preferred_element_type=jnp.float32,
    )
    summed = lax.psum_scatter(partial_sums, HEAD, scatter_dimension=0, tiled=True)
    quarter = summed.shape[0]
    quarter_slots = lax.dynamic_slice_in_dim(
        slot_request, lax.axis_index(HEAD) * quarter, quarter, 0
    )
    attended = (jnp.take(residual, quarter_slots, axis=0).astype(jnp.float32) + summed).astype(
        jnp.bfloat16
    )
    column_width = attended.shape[1]
    widened = attended.astype(jnp.float32)
    partial_squares = jnp.sum(widened * widened, axis=1)
    high = partial_squares.astype(jnp.bfloat16)
    low = (partial_squares - high.astype(jnp.float32)).astype(jnp.bfloat16)
    pad_rows = SQ_ROWS - 2
    block_t = jnp.concatenate(
        [attended.T, high[None], low[None], jnp.zeros((pad_rows, quarter), jnp.bfloat16)], axis=0
    )
    hidden_t = lax.all_gather(block_t[None], REQ + (HEAD,), axis=0, tiled=True).reshape(
        req_count, head_count, column_width + SQ_ROWS, quarter
    )
    col_block = gate_proj.shape[1]
    gain = norm_gain.astype(jnp.float32)[:, None]
    padded = -(-col_block // 8) * 8

    def prepared(weights):
        scaled_w = (weights.astype(jnp.float32) * gain).astype(jnp.bfloat16)
        shaped_w = scaled_w.reshape(req_count, column_width, col_block).transpose(0, 2, 1)
        return jnp.pad(shaped_w, ((0, 0), (0, padded - col_block), (0, 0)))

    weights_t = jnp.concatenate([prepared(gate_proj), prepared(up_proj)], axis=1)
    active_t = gate_up(hidden_t, weights_t, col_block)
    active_all = lax.all_gather(active_t, HEAD, axis=0, tiled=True)
    down_sums = lax.dot_general(
        active_all, down_proj, (((0,), (0,)), ((), ())), preferred_element_type=jnp.float32
    )
    cores = lax.axis_size(CORE)
    chips = req_count // cores
    pieces = down_sums.astype(jnp.bfloat16).reshape(chips, cores, owned, down_sums.shape[1])
    on_chip = lax.all_to_all(pieces, CORE, 1, 1, tiled=True)
    chip_sums = jnp.sum(on_chip.astype(jnp.float32), axis=1).astype(jnp.bfloat16)
    received = lax.all_to_all(chip_sums, CHIPS, 0, 0, tiled=True)
    ffn_out = jnp.sum(received.astype(jnp.float32), axis=0).astype(jnp.bfloat16)
    return (attended, ffn_out)


def solution(mesh):
    placed = (
        P(REQ, HEAD),
        P(REQ, HEAD),
        P(REQ, HEAD),
        P(REQ, HEAD),
        P(REQ, HEAD),
        P(),
        P(),
        P(None, REQ),
        P(HEAD, REQ),
        P(),
        P(None, REQ + (HEAD,)),
        P(None, REQ + (HEAD,)),
        P(REQ, HEAD),
    )
    req_size, head_size = mesh.devices.shape
    named = jax.sharding.Mesh(
        mesh.devices.reshape(req_size // CORES_PER_CHIP, CORES_PER_CHIP, head_size),
        (CHIPS, CORE, HEAD),
    )
    return jax.shard_map(
        body,
        mesh=named,
        in_specs=placed,
        out_specs=(P(HEAD, REQ), P(REQ, HEAD)),
        check_vma=False,
    )
```

```python
import math

import jax
import jax.numpy as jnp
from jax import lax
from jax.experimental import pallas as pl
from jax.experimental.pallas import tpu as pltpu
from jax.sharding import PartitionSpec as P

D = 5120
HD = 128
CHIP_AXES = ("z", "x")
CORE = "core"
REQ = CHIP_AXES + (CORE,)
CORES_PER_CHIP = 2
X_CHIPS = 4
HEAD = "y"
HEADS_PER_STEP = 2
R_PER_STEP = 8
SQ_ROWS = 16


def rope_tables(positions):
    half_dim = HD // 2
    freq_steps = jnp.arange(half_dim, dtype=jnp.float32)
    inverse = jnp.exp(freq_steps * (-2.0 * math.log(10000.0) / HD))
    angles = positions.astype(jnp.float32)[:, None] * inverse[None, :]
    return (jnp.cos(angles), jnp.sin(angles))


def rotate_half(vectors, cosine, sine_table):
    half_dim = HD // 2
    first_half = vectors[..., :half_dim]
    second = vectors[..., half_dim:]
    cos_grid = cosine[:, None, :]
    sin_grid = sine_table[:, None, :]
    return jnp.concatenate(
        [first_half * cos_grid - second * sin_grid, second * cos_grid + first_half * sin_grid],
        axis=-1,
    )


def attention_kernel(start_ref, end_ref, q_ref, k_ref, vn_ref, kp_ref, vp_ref, o_ref):
    score_scale = HD ** (-0.5)
    slots = q_ref.shape[0]
    rows = kp_ref.shape[0]
    places = lax.broadcasted_iota(jnp.int32, (slots, rows), 1)
    member = (places >= start_ref[...]) & (places < end_ref[...])
    for j in range(HEADS_PER_STEP):
        cols = slice(j * HD, (j + 1) * HD)
        query = q_ref[:, cols]
        scores = (
            lax.dot_general(
                query,
                kp_ref[:, cols],
                (((1,), (1,)), ((), ())),
                preferred_element_type=jnp.float32,
            )
            * score_scale
        )
        own_score = (
            jnp.sum(
                query.astype(jnp.float32) * k_ref[:, cols].astype(jnp.float32),
                axis=-1,
                keepdims=True,
            )
            * score_scale
        )
        masked = jnp.where(member, scores, -jnp.inf)
        row_top = jnp.maximum(jnp.max(masked, axis=-1, keepdims=True), own_score)
        weights = jnp.where(member, jnp.exp(scores - row_top), 0.0)
        own_weight = jnp.exp(own_score - row_top)
        row_total = jnp.sum(weights, axis=-1, keepdims=True) + own_weight
        summed = jnp.dot(
            weights.astype(jnp.bfloat16), vp_ref[:, cols], preferred_element_type=jnp.float32
        )
        own_bf = own_weight.astype(jnp.bfloat16).astype(jnp.float32)
        summed = summed + own_bf * vn_ref[:, cols].astype(jnp.float32)
        o_ref[:, cols] = (summed / row_total).astype(o_ref.dtype)


def attend_local(query_rot, key_rot, value_new, key_pool, value_pool, starts, ends):
    slots, width = query_rot.shape
    rows = key_pool.shape[0]
    block = HEADS_PER_STEP * HD
    steps = width // block
    slot_spec = pl.BlockSpec((slots, block), lambda g: (0, g))
    pool_spec = pl.BlockSpec((rows, block), lambda g: (0, g))
    bound_spec = pl.BlockSpec((slots, 1), lambda g: (0, 0))
    flops = 4 * slots * rows * width
    return pl.pallas_call(
        attention_kernel,
        grid=(steps,),
        in_specs=[bound_spec, bound_spec, slot_spec, slot_spec, slot_spec, pool_spec, pool_spec],
        out_specs=slot_spec,
        out_shape=jax.ShapeDtypeStruct((slots, width), jnp.bfloat16),
        cost_estimate=pl.CostEstimate(
            flops=flops,
            transcendentals=slots * rows * (width // HD),
            bytes_accessed=2 * rows * width * 2 + 4 * slots * width * 2,
        ),
    )(starts, ends, query_rot, key_rot, value_new, key_pool, value_pool)


def gate_up_kernel(x_ref, w_ref, o_ref, acc, acc_sq):
    step = pl.program_id(0)
    quarters = x_ref.shape[1]
    width = x_ref.shape[3]
    columns = w_ref.shape[2]
    half = w_ref.shape[1] // 2
    units = o_ref.shape[0]

    @pl.when(step == 0)
    def _():
        acc[...] = jnp.zeros_like(acc)
        acc_sq[...] = jnp.zeros_like(acc_sq)

    def body(i, carry):
        weights = w_ref[i]
        for quarter in range(quarters):
            cols = slice(quarter * width, (quarter + 1) * width)
            block = x_ref[i, quarter, :columns, :]
            acc[:, cols] += jnp.dot(weights, block, preferred_element_type=jnp.float32)
            acc_sq[:, cols] += x_ref[i, quarter, columns:, :].astype(jnp.float32)
        return carry

    lax.fori_loop(0, x_ref.shape[0], body, 0)

    @pl.when(step == pl.num_programs(0) - 1)
    def _():
        squares = acc_sq[0:1, :] + acc_sq[1:2, :]
        inverse = lax.rsqrt(squares / D + 1e-05)
        gate_pre = acc[:half, :] * inverse
        silu = gate_pre / (1.0 + jnp.exp(-gate_pre))
        active = silu * (acc[half:, :] * inverse)
        o_ref[...] = active[:units].astype(o_ref.dtype)


def gate_up(hidden_t, weights_t, units):
    chunks, quarters, rows, width = hidden_t.shape
    both, columns = weights_t.shape[1], weights_t.shape[2]
    slots = quarters * width
    return pl.pallas_call(
        gate_up_kernel,
        grid=(chunks // R_PER_STEP,),
        in_specs=[
            pl.BlockSpec((R_PER_STEP, quarters, rows, width), lambda s: (s, 0, 0, 0)),
            pl.BlockSpec((R_PER_STEP, both, columns), lambda s: (s, 0, 0)),
        ],
        out_specs=pl.BlockSpec((units, slots), lambda s: (0, 0)),
        out_shape=jax.ShapeDtypeStruct((units, slots), jnp.bfloat16),
        scratch_shapes=[
            pltpu.VMEM((both, slots), jnp.float32),
            pltpu.VMEM((rows - columns, slots), jnp.float32),
        ],
        compiler_params=pltpu.CompilerParams(dimension_semantics=("arbitrary",)),
        cost_estimate=pl.CostEstimate(
            flops=2 * both * slots * chunks * columns,
            transcendentals=units * slots,
            bytes_accessed=hidden_t.size * 2 + weights_t.size * 2 + units * slots * 2,
        ),
    )(hidden_t, weights_t)


def body(
    query_new,
    key_new,
    value_new,
    key_pool,
    value_pool,
    lengths,
    slot_request,
    residual,
    out_proj,
    norm_gain,
    gate_proj,
    up_proj,
    down_proj,
):
    owned = query_new.shape[0]
    groups = query_new.shape[1] // HD
    req_count = lax.axis_size(REQ)
    head_count = lax.axis_size(HEAD)
    first_slot = lax.axis_index(REQ) * owned
    my_requests = lax.dynamic_slice_in_dim(slot_request, first_slot, owned, 0)
    my_lengths = jnp.take(lengths, my_requests, axis=0)
    cosine, sine_table = rope_tables(my_lengths)
    shaped = (owned, groups, HD)
    query_rot = rotate_half(
        query_new.astype(jnp.float32).reshape(shaped), cosine, sine_table
    ).astype(jnp.bfloat16)
    key_rot = rotate_half(key_new.astype(jnp.float32).reshape(shaped), cosine, sine_table).astype(
        jnp.bfloat16
    )
    seg_ends = jnp.cumsum(my_lengths)
    starts = (seg_ends - my_lengths).astype(jnp.int32)
    attention = attend_local(
        query_rot.reshape(owned, groups * HD),
        key_rot.reshape(owned, groups * HD),
        value_new,
        key_pool,
        value_pool,
        starts[:, None],
        seg_ends.astype(jnp.int32)[:, None],
    )
    partial_sums = jnp.dot(
        lax.all_gather(attention, REQ, axis=0, tiled=True),
        out_proj,
        preferred_element_type=jnp.float32,
    )
    summed = lax.psum_scatter(partial_sums, HEAD, scatter_dimension=0, tiled=True)
    quarter = summed.shape[0]
    quarter_slots = lax.dynamic_slice_in_dim(
        slot_request, lax.axis_index(HEAD) * quarter, quarter, 0
    )
    attended = (jnp.take(residual, quarter_slots, axis=0).astype(jnp.float32) + summed).astype(
        jnp.bfloat16
    )
    column_width = attended.shape[1]
    widened = attended.astype(jnp.float32)
    partial_squares = jnp.sum(widened * widened, axis=1)
    high = partial_squares.astype(jnp.bfloat16)
    low = (partial_squares - high.astype(jnp.float32)).astype(jnp.bfloat16)
    pad_rows = SQ_ROWS - 2
    block_t = jnp.concatenate(
        [attended.T, high[None], low[None], jnp.zeros((pad_rows, quarter), jnp.bfloat16)], axis=0
    )
    hidden_t = lax.all_gather(block_t[None], REQ + (HEAD,), axis=0, tiled=True).reshape(
        req_count, head_count, column_width + SQ_ROWS, quarter
    )
    col_block = gate_proj.shape[1]
    gain = norm_gain.astype(jnp.float32)[:, None]
    padded = -(-col_block // 8) * 8

    def prepared(weights):
        scaled_w = (weights.astype(jnp.float32) * gain).astype(jnp.bfloat16)
        shaped_w = scaled_w.reshape(req_count, column_width, col_block).transpose(0, 2, 1)
        return jnp.pad(shaped_w, ((0, 0), (0, padded - col_block), (0, 0)))

    weights_t = jnp.concatenate([prepared(gate_proj), prepared(up_proj)], axis=1)
    active_t = gate_up(hidden_t, weights_t, col_block)
    active_all = lax.all_gather(active_t, HEAD, axis=0, tiled=True)
    down_sums = lax.dot_general(
        active_all, down_proj, (((0,), (0,)), ((), ())), preferred_element_type=jnp.float32
    )
    width = down_sums.shape[1]
    stages = (CORE,) + CHIP_AXES[::-1]
    sizes = [lax.axis_size(name) for name in REQ]
    running = down_sums.astype(jnp.bfloat16).reshape(*sizes, owned, width)
    for name in stages:
        place = REQ.index(name)
        swapped = lax.all_to_all(running, name, place, place, tiled=True)
        running = jnp.sum(swapped.astype(jnp.float32), axis=place).astype(jnp.bfloat16)
    ffn_out = running
    return (attended, ffn_out)


def solution(mesh):
    placed = (
        P(REQ, HEAD),
        P(REQ, HEAD),
        P(REQ, HEAD),
        P(REQ, HEAD),
        P(REQ, HEAD),
        P(),
        P(),
        P(None, REQ),
        P(HEAD, REQ),
        P(),
        P(None, REQ + (HEAD,)),
        P(None, REQ + (HEAD,)),
        P(REQ, HEAD),
    )
    req_size, head_size = mesh.devices.shape
    z_chips = req_size // (CORES_PER_CHIP * X_CHIPS)
    named = jax.sharding.Mesh(
        mesh.devices.reshape(z_chips, X_CHIPS, CORES_PER_CHIP, head_size),
        CHIP_AXES + (CORE, HEAD),
    )
    return jax.shard_map(
        body,
        mesh=named,
        in_specs=placed,
        out_specs=(P(HEAD, REQ), P(REQ, HEAD)),
        check_vma=False,
    )
```

```python
import math

import jax
import jax.numpy as jnp
from jax import lax
from jax.experimental import pallas as pl
from jax.experimental.pallas import tpu as pltpu
from jax.sharding import PartitionSpec as P

D = 5120
HD = 128
CHIPS = "chip"
CORE = "core"
REQ = (CHIPS, CORE)
CORES_PER_CHIP = 2
HEAD = "y"
HEADS_PER_STEP = 2
R_PER_STEP = 8
SQ_ROWS = 16


def rope_tables(positions):
    half_dim = HD // 2
    freq_steps = jnp.arange(half_dim, dtype=jnp.float32)
    inverse = jnp.exp(freq_steps * (-2.0 * math.log(10000.0) / HD))
    angles = positions.astype(jnp.float32)[:, None] * inverse[None, :]
    return (jnp.cos(angles), jnp.sin(angles))


def rotate_half(vectors, cosine, sine_table):
    half_dim = HD // 2
    first_half = vectors[..., :half_dim]
    second = vectors[..., half_dim:]
    cos_grid = cosine[:, None, :]
    sin_grid = sine_table[:, None, :]
    return jnp.concatenate(
        [first_half * cos_grid - second * sin_grid, second * cos_grid + first_half * sin_grid],
        axis=-1,
    )


def attention_kernel(start_ref, end_ref, q_ref, k_ref, vn_ref, kp_ref, vp_ref, o_ref):
    score_scale = HD ** (-0.5)
    slots = q_ref.shape[0]
    rows = kp_ref.shape[0]
    places = lax.broadcasted_iota(jnp.int32, (slots, rows), 1)
    member = (places >= start_ref[...]) & (places < end_ref[...])
    for j in range(HEADS_PER_STEP):
        cols = slice(j * HD, (j + 1) * HD)
        query = q_ref[:, cols]
        scores = (
            lax.dot_general(
                query,
                kp_ref[:, cols],
                (((1,), (1,)), ((), ())),
                preferred_element_type=jnp.float32,
            )
            * score_scale
        )
        own_score = (
            jnp.sum(
                query.astype(jnp.float32) * k_ref[:, cols].astype(jnp.float32),
                axis=-1,
                keepdims=True,
            )
            * score_scale
        )
        masked = jnp.where(member, scores, -jnp.inf)
        row_top = jnp.maximum(jnp.max(masked, axis=-1, keepdims=True), own_score)
        weights = jnp.where(member, jnp.exp(scores - row_top), 0.0)
        own_weight = jnp.exp(own_score - row_top)
        row_total = jnp.sum(weights, axis=-1, keepdims=True) + own_weight
        summed = jnp.dot(
            weights.astype(jnp.bfloat16), vp_ref[:, cols], preferred_element_type=jnp.float32
        )
        own_bf = own_weight.astype(jnp.bfloat16).astype(jnp.float32)
        summed = summed + own_bf * vn_ref[:, cols].astype(jnp.float32)
        o_ref[:, cols] = (summed / row_total).astype(o_ref.dtype)


def attend_local(query_rot, key_rot, value_new, key_pool, value_pool, starts, ends):
    slots, width = query_rot.shape
    rows = key_pool.shape[0]
    block = HEADS_PER_STEP * HD
    steps = width // block
    slot_spec = pl.BlockSpec((slots, block), lambda g: (0, g))
    pool_spec = pl.BlockSpec((rows, block), lambda g: (0, g))
    bound_spec = pl.BlockSpec((slots, 1), lambda g: (0, 0))
    flops = 4 * slots * rows * width
    return pl.pallas_call(
        attention_kernel,
        grid=(steps,),
        in_specs=[bound_spec, bound_spec, slot_spec, slot_spec, slot_spec, pool_spec, pool_spec],
        out_specs=slot_spec,
        out_shape=jax.ShapeDtypeStruct((slots, width), jnp.bfloat16),
        cost_estimate=pl.CostEstimate(
            flops=flops,
            transcendentals=slots * rows * (width // HD),
            bytes_accessed=2 * rows * width * 2 + 4 * slots * width * 2,
        ),
    )(starts, ends, query_rot, key_rot, value_new, key_pool, value_pool)


def gate_up_kernel(x_ref, w_ref, o_ref, acc, acc_sq):
    step = pl.program_id(0)
    quarters = x_ref.shape[1]
    width = x_ref.shape[3]
    columns = w_ref.shape[2]
    half = w_ref.shape[1] // 2
    units = o_ref.shape[0]

    @pl.when(step == 0)
    def _():
        acc[...] = jnp.zeros_like(acc)
        acc_sq[...] = jnp.zeros_like(acc_sq)

    def body(i, carry):
        weights = w_ref[i]
        for quarter in range(quarters):
            cols = slice(quarter * width, (quarter + 1) * width)
            block = x_ref[i, quarter, :columns, :]
            acc[:, cols] += jnp.dot(weights, block, preferred_element_type=jnp.float32)
            acc_sq[:, cols] += x_ref[i, quarter, columns:, :].astype(jnp.float32)
        return carry

    lax.fori_loop(0, x_ref.shape[0], body, 0)

    @pl.when(step == pl.num_programs(0) - 1)
    def _():
        squares = acc_sq[0:1, :] + acc_sq[1:2, :]
        inverse = lax.rsqrt(squares / D + 1e-05)
        gate_pre = acc[:half, :] * inverse
        silu = gate_pre / (1.0 + jnp.exp(-gate_pre))
        active = silu * (acc[half:, :] * inverse)
        o_ref[...] = active[:units].astype(o_ref.dtype)


def gate_up(hidden_t, weights_t, units):
    chunks, quarters, rows, width = hidden_t.shape
    both, columns = weights_t.shape[1], weights_t.shape[2]
    slots = quarters * width
    return pl.pallas_call(
        gate_up_kernel,
        grid=(chunks // R_PER_STEP,),
        in_specs=[
            pl.BlockSpec((R_PER_STEP, quarters, rows, width), lambda s: (s, 0, 0, 0)),
            pl.BlockSpec((R_PER_STEP, both, columns), lambda s: (s, 0, 0)),
        ],
        out_specs=pl.BlockSpec((units, slots), lambda s: (0, 0)),
        out_shape=jax.ShapeDtypeStruct((units, slots), jnp.bfloat16),
        scratch_shapes=[
            pltpu.VMEM((both, slots), jnp.float32),
            pltpu.VMEM((rows - columns, slots), jnp.float32),
        ],
        compiler_params=pltpu.CompilerParams(dimension_semantics=("arbitrary",)),
        cost_estimate=pl.CostEstimate(
            flops=2 * both * slots * chunks * columns,
            transcendentals=units * slots,
            bytes_accessed=hidden_t.size * 2 + weights_t.size * 2 + units * slots * 2,
        ),
    )(hidden_t, weights_t)


def body(
    query_new,
    key_new,
    value_new,
    key_pool,
    value_pool,
    lengths,
    slot_request,
    residual,
    out_proj,
    norm_gain,
    gate_proj,
    up_proj,
    down_proj,
):
    owned = query_new.shape[0]
    groups = query_new.shape[1] // HD
    req_count = lax.axis_size(REQ)
    head_count = lax.axis_size(HEAD)
    first_slot = lax.axis_index(REQ) * owned
    my_requests = lax.dynamic_slice_in_dim(slot_request, first_slot, owned, 0)
    my_lengths = jnp.take(lengths, my_requests, axis=0)
    cosine, sine_table = rope_tables(my_lengths)
    shaped = (owned, groups, HD)
    query_rot = rotate_half(
        query_new.astype(jnp.float32).reshape(shaped), cosine, sine_table
    ).astype(jnp.bfloat16)
    key_rot = rotate_half(key_new.astype(jnp.float32).reshape(shaped), cosine, sine_table).astype(
        jnp.bfloat16
    )
    seg_ends = jnp.cumsum(my_lengths)
    starts = (seg_ends - my_lengths).astype(jnp.int32)
    attention = attend_local(
        query_rot.reshape(owned, groups * HD),
        key_rot.reshape(owned, groups * HD),
        value_new,
        key_pool,
        value_pool,
        starts[:, None],
        seg_ends.astype(jnp.int32)[:, None],
    )
    partial_sums = jnp.dot(
        lax.all_gather(attention, REQ, axis=0, tiled=True),
        out_proj,
        preferred_element_type=jnp.float32,
    )
    summed = lax.psum_scatter(partial_sums, HEAD, scatter_dimension=0, tiled=True)
    quarter = summed.shape[0]
    quarter_slots = lax.dynamic_slice_in_dim(
        slot_request, lax.axis_index(HEAD) * quarter, quarter, 0
    )
    attended = (jnp.take(residual, quarter_slots, axis=0).astype(jnp.float32) + summed).astype(
        jnp.bfloat16
    )
    column_width = attended.shape[1]
    widened = attended.astype(jnp.float32)
    partial_squares = jnp.sum(widened * widened, axis=1)
    high = partial_squares.astype(jnp.bfloat16)
    low = (partial_squares - high.astype(jnp.float32)).astype(jnp.bfloat16)
    pad_rows = SQ_ROWS - 2
    block_t = jnp.concatenate(
        [attended.T, high[None], low[None], jnp.zeros((pad_rows, quarter), jnp.bfloat16)], axis=0
    )
    hidden_t = lax.all_gather(block_t[None], REQ + (HEAD,), axis=0, tiled=True).reshape(
        req_count, head_count, column_width + SQ_ROWS, quarter
    )
    col_block = gate_proj.shape[1]
    gain = norm_gain.astype(jnp.float32)[:, None]
    padded = -(-col_block // 8) * 8

    def prepared(weights):
        scaled_w = (weights.astype(jnp.float32) * gain).astype(jnp.bfloat16)
        shaped_w = scaled_w.reshape(req_count, column_width, col_block).transpose(0, 2, 1)
        return jnp.pad(shaped_w, ((0, 0), (0, padded - col_block), (0, 0)))

    weights_t = jnp.concatenate([prepared(gate_proj), prepared(up_proj)], axis=1)
    active_t = gate_up(hidden_t, weights_t, col_block)
    active_all = lax.all_gather(active_t, HEAD, axis=0, tiled=True)
    down_sums = lax.dot_general(
        active_all, down_proj, (((0,), (0,)), ((), ())), preferred_element_type=jnp.float32
    )
    cores = lax.axis_size(CORE)
    chips = req_count // cores
    pieces = down_sums.astype(jnp.bfloat16).reshape(chips, cores, owned, down_sums.shape[1])
    my_core = lax.axis_index(CORE)
    kept = lax.dynamic_index_in_dim(pieces, my_core, axis=1, keepdims=False)
    sent = lax.dynamic_index_in_dim(pieces, cores - 1 - my_core, axis=1, keepdims=False)
    arrived = lax.ppermute(sent, CORE, [(core, cores - 1 - core) for core in range(cores)])
    chip_sums = (kept.astype(jnp.float32) + arrived.astype(jnp.float32)).astype(jnp.bfloat16)
    received = lax.all_to_all(chip_sums, CHIPS, 0, 0, tiled=True)
    ffn_out = jnp.sum(received.astype(jnp.float32), axis=0).astype(jnp.bfloat16)
    return (attended, ffn_out)


def solution(mesh):
    placed = (
        P(REQ, HEAD),
        P(REQ, HEAD),
        P(REQ, HEAD),
        P(REQ, HEAD),
        P(REQ, HEAD),
        P(),
        P(),
        P(None, REQ),
        P(HEAD, REQ),
        P(),
        P(None, REQ + (HEAD,)),
        P(None, REQ + (HEAD,)),
        P(REQ, HEAD),
    )
    req_size, head_size = mesh.devices.shape
    named = jax.sharding.Mesh(
        mesh.devices.reshape(req_size // CORES_PER_CHIP, CORES_PER_CHIP, head_size),
        (CHIPS, CORE, HEAD),
    )
    return jax.shard_map(
        body,
        mesh=named,
        in_specs=placed,
        out_specs=(P(HEAD, REQ), P(REQ, HEAD)),
        check_vma=False,
    )
```

```python
import math

import jax
import jax.numpy as jnp
from jax import lax
from jax.experimental import pallas as pl
from jax.experimental.pallas import tpu as pltpu
from jax.sharding import PartitionSpec as P

D = 5120
HD = 128
CHIPS = "chip"
CORE = "core"
REQ = (CHIPS, CORE)
CORES_PER_CHIP = 2
HEAD = "y"
HEADS_PER_STEP = 2
R_PER_STEP = 8
SQ_ROWS = 16


def rope_tables(positions):
    half_dim = HD // 2
    freq_steps = jnp.arange(half_dim, dtype=jnp.float32)
    inverse = jnp.exp(freq_steps * (-2.0 * math.log(10000.0) / HD))
    angles = positions.astype(jnp.float32)[:, None] * inverse[None, :]
    return (jnp.cos(angles), jnp.sin(angles))


def rotate_half(vectors, cosine, sine_table):
    half_dim = HD // 2
    first_half = vectors[..., :half_dim]
    second = vectors[..., half_dim:]
    cos_grid = cosine[:, None, :]
    sin_grid = sine_table[:, None, :]
    return jnp.concatenate(
        [first_half * cos_grid - second * sin_grid, second * cos_grid + first_half * sin_grid],
        axis=-1,
    )


def attention_kernel(start_ref, end_ref, q_ref, k_ref, vn_ref, kp_ref, vp_ref, o_ref):
    score_scale = HD ** (-0.5)
    slots = q_ref.shape[0]
    rows = kp_ref.shape[0]
    places = lax.broadcasted_iota(jnp.int32, (slots, rows), 1)
    member = (places >= start_ref[...]) & (places < end_ref[...])
    for j in range(HEADS_PER_STEP):
        cols = slice(j * HD, (j + 1) * HD)
        query = q_ref[:, cols]
        scores = (
            lax.dot_general(
                query,
                kp_ref[:, cols],
                (((1,), (1,)), ((), ())),
                preferred_element_type=jnp.float32,
            )
            * score_scale
        )
        own_score = (
            jnp.sum(
                query.astype(jnp.float32) * k_ref[:, cols].astype(jnp.float32),
                axis=-1,
                keepdims=True,
            )
            * score_scale
        )
        masked = jnp.where(member, scores, -jnp.inf)
        row_top = jnp.maximum(jnp.max(masked, axis=-1, keepdims=True), own_score)
        weights = jnp.where(member, jnp.exp(scores - row_top), 0.0)
        own_weight = jnp.exp(own_score - row_top)
        row_total = jnp.sum(weights, axis=-1, keepdims=True) + own_weight
        summed = jnp.dot(
            weights.astype(jnp.bfloat16), vp_ref[:, cols], preferred_element_type=jnp.float32
        )
        own_bf = own_weight.astype(jnp.bfloat16).astype(jnp.float32)
        summed = summed + own_bf * vn_ref[:, cols].astype(jnp.float32)
        o_ref[:, cols] = (summed / row_total).astype(o_ref.dtype)


def attend_local(query_rot, key_rot, value_new, key_pool, value_pool, starts, ends):
    slots, width = query_rot.shape
    rows = key_pool.shape[0]
    block = HEADS_PER_STEP * HD
    steps = width // block
    slot_spec = pl.BlockSpec((slots, block), lambda g: (0, g))
    pool_spec = pl.BlockSpec((rows, block), lambda g: (0, g))
    bound_spec = pl.BlockSpec((slots, 1), lambda g: (0, 0))
    flops = 4 * slots * rows * width
    return pl.pallas_call(
        attention_kernel,
        grid=(steps,),
        in_specs=[bound_spec, bound_spec, slot_spec, slot_spec, slot_spec, pool_spec, pool_spec],
        out_specs=slot_spec,
        out_shape=jax.ShapeDtypeStruct((slots, width), jnp.bfloat16),
        cost_estimate=pl.CostEstimate(
            flops=flops,
            transcendentals=slots * rows * (width // HD),
            bytes_accessed=2 * rows * width * 2 + 4 * slots * width * 2,
        ),
    )(starts, ends, query_rot, key_rot, value_new, key_pool, value_pool)


def gate_up_kernel(x_ref, w_ref, o_ref, acc, acc_sq):
    step = pl.program_id(0)
    quarters = x_ref.shape[1]
    width = x_ref.shape[3]
    columns = w_ref.shape[2]
    half = w_ref.shape[1] // 2
    units = o_ref.shape[0]

    @pl.when(step == 0)
    def _():
        acc[...] = jnp.zeros_like(acc)
        acc_sq[...] = jnp.zeros_like(acc_sq)

    def body(i, carry):
        weights = w_ref[i]
        for quarter in range(quarters):
            cols = slice(quarter * width, (quarter + 1) * width)
            block = x_ref[i, quarter, :columns, :]
            acc[:, cols] += jnp.dot(weights, block, preferred_element_type=jnp.float32)
            acc_sq[:, cols] += x_ref[i, quarter, columns:, :].astype(jnp.float32)
        return carry

    lax.fori_loop(0, x_ref.shape[0], body, 0)

    @pl.when(step == pl.num_programs(0) - 1)
    def _():
        squares = acc_sq[0:1, :] + acc_sq[1:2, :]
        inverse = lax.rsqrt(squares / D + 1e-05)
        gate_pre = acc[:half, :] * inverse
        silu = gate_pre / (1.0 + jnp.exp(-gate_pre))
        active = silu * (acc[half:, :] * inverse)
        o_ref[...] = active[:units].astype(o_ref.dtype)


def gate_up(hidden_t, weights_t, units):
    chunks, quarters, rows, width = hidden_t.shape
    both, columns = weights_t.shape[1], weights_t.shape[2]
    slots = quarters * width
    return pl.pallas_call(
        gate_up_kernel,
        grid=(chunks // R_PER_STEP,),
        in_specs=[
            pl.BlockSpec((R_PER_STEP, quarters, rows, width), lambda s: (s, 0, 0, 0)),
            pl.BlockSpec((R_PER_STEP, both, columns), lambda s: (s, 0, 0)),
        ],
        out_specs=pl.BlockSpec((units, slots), lambda s: (0, 0)),
        out_shape=jax.ShapeDtypeStruct((units, slots), jnp.bfloat16),
        scratch_shapes=[
            pltpu.VMEM((both, slots), jnp.float32),
            pltpu.VMEM((rows - columns, slots), jnp.float32),
        ],
        compiler_params=pltpu.CompilerParams(dimension_semantics=("arbitrary",)),
        cost_estimate=pl.CostEstimate(
            flops=2 * both * slots * chunks * columns,
            transcendentals=units * slots,
            bytes_accessed=hidden_t.size * 2 + weights_t.size * 2 + units * slots * 2,
        ),
    )(hidden_t, weights_t)


def body(
    query_new,
    key_new,
    value_new,
    key_pool,
    value_pool,
    lengths,
    slot_request,
    residual,
    out_proj,
    norm_gain,
    gate_proj,
    up_proj,
    down_proj,
):
    owned = query_new.shape[0]
    groups = query_new.shape[1] // HD
    req_count = lax.axis_size(REQ)
    head_count = lax.axis_size(HEAD)
    first_slot = lax.axis_index(REQ) * owned
    my_requests = lax.dynamic_slice_in_dim(slot_request, first_slot, owned, 0)
    my_lengths = jnp.take(lengths, my_requests, axis=0)
    cosine, sine_table = rope_tables(my_lengths)
    shaped = (owned, groups, HD)
    query_rot = rotate_half(
        query_new.astype(jnp.float32).reshape(shaped), cosine, sine_table
    ).astype(jnp.bfloat16)
    key_rot = rotate_half(key_new.astype(jnp.float32).reshape(shaped), cosine, sine_table).astype(
        jnp.bfloat16
    )
    seg_ends = jnp.cumsum(my_lengths)
    starts = (seg_ends - my_lengths).astype(jnp.int32)
    attention = attend_local(
        query_rot.reshape(owned, groups * HD),
        key_rot.reshape(owned, groups * HD),
        value_new,
        key_pool,
        value_pool,
        starts[:, None],
        seg_ends.astype(jnp.int32)[:, None],
    )
    partial_sums = jnp.dot(
        lax.all_gather(attention, REQ, axis=0, tiled=True),
        out_proj,
        preferred_element_type=jnp.float32,
    )
    summed = lax.psum_scatter(partial_sums, HEAD, scatter_dimension=0, tiled=True)
    quarter = summed.shape[0]
    quarter_slots = lax.dynamic_slice_in_dim(
        slot_request, lax.axis_index(HEAD) * quarter, quarter, 0
    )
    attended = (jnp.take(residual, quarter_slots, axis=0).astype(jnp.float32) + summed).astype(
        jnp.bfloat16
    )
    column_width = attended.shape[1]
    widened = attended.astype(jnp.float32)
    partial_squares = jnp.sum(widened * widened, axis=1)
    high = partial_squares.astype(jnp.bfloat16)
    low = (partial_squares - high.astype(jnp.float32)).astype(jnp.bfloat16)
    pad_rows = SQ_ROWS - 2
    block_t = jnp.concatenate(
        [attended.T, high[None], low[None], jnp.zeros((pad_rows, quarter), jnp.bfloat16)], axis=0
    )
    hidden_t = lax.all_gather(block_t[None], REQ + (HEAD,), axis=0, tiled=True).reshape(
        req_count, head_count, column_width + SQ_ROWS, quarter
    )
    col_block = gate_proj.shape[1]
    gain = norm_gain.astype(jnp.float32)[:, None]
    padded = -(-col_block // 8) * 8

    def prepared(weights):
        scaled_w = (weights.astype(jnp.float32) * gain).astype(jnp.bfloat16)
        shaped_w = scaled_w.reshape(req_count, column_width, col_block).transpose(0, 2, 1)
        return jnp.pad(shaped_w, ((0, 0), (0, padded - col_block), (0, 0)))

    weights_t = jnp.concatenate([prepared(gate_proj), prepared(up_proj)], axis=1)
    active_t = gate_up(hidden_t, weights_t, col_block)
    active_all = lax.all_gather(active_t, HEAD, axis=0, tiled=True)
    down_sums = lax.dot_general(
        active_all, down_proj, (((0,), (0,)), ((), ())), preferred_element_type=jnp.float32
    )
    cores = lax.axis_size(CORE)
    chips = req_count // cores
    pieces = down_sums.astype(jnp.bfloat16).reshape(chips, cores, owned, down_sums.shape[1])
    my_core = lax.axis_index(CORE)
    kept = lax.dynamic_index_in_dim(pieces, my_core, axis=1, keepdims=False)
    sent = lax.dynamic_index_in_dim(pieces, cores - 1 - my_core, axis=1, keepdims=False)
    arrived = lax.ppermute(sent, CORE, [(core, cores - 1 - core) for core in range(cores)])
    chip_sums = (kept.astype(jnp.float32) + arrived.astype(jnp.float32)).astype(jnp.bfloat16)
    my_chip = lax.axis_index(CHIPS)
    order = (my_chip + jnp.arange(chips, dtype=jnp.int32)) % chips
    rolled = jnp.take(chip_sums, order, axis=0)
    total = rolled[0].astype(jnp.float32)
    for shift in range(1, chips):
        pairs = [(chip, (chip + shift) % chips) for chip in range(chips)]
        total = total + lax.ppermute(rolled[shift], CHIPS, pairs).astype(jnp.float32)
    ffn_out = total.astype(jnp.bfloat16)
    return (attended, ffn_out)


def solution(mesh):
    placed = (
        P(REQ, HEAD),
        P(REQ, HEAD),
        P(REQ, HEAD),
        P(REQ, HEAD),
        P(REQ, HEAD),
        P(),
        P(),
        P(None, REQ),
        P(HEAD, REQ),
        P(),
        P(None, REQ + (HEAD,)),
        P(None, REQ + (HEAD,)),
        P(REQ, HEAD),
    )
    req_size, head_size = mesh.devices.shape
    named = jax.sharding.Mesh(
        mesh.devices.reshape(req_size // CORES_PER_CHIP, CORES_PER_CHIP, head_size),
        (CHIPS, CORE, HEAD),
    )
    return jax.shard_map(
        body,
        mesh=named,
        in_specs=placed,
        out_specs=(P(HEAD, REQ), P(REQ, HEAD)),
        check_vma=False,
    )
```

```python
import math

import jax
import jax.numpy as jnp
from jax import lax
from jax.experimental import pallas as pl
from jax.experimental.pallas import tpu as pltpu
from jax.sharding import PartitionSpec as P

D = 5120
HD = 128
CHIPS = "chip"
CORE = "core"
REQ = (CHIPS, CORE)
CORES_PER_CHIP = 2
HEAD = "y"
HEADS_PER_STEP = 2
R_PER_STEP = 8
SQ_ROWS = 16


def rope_tables(positions):
    half_dim = HD // 2
    freq_steps = jnp.arange(half_dim, dtype=jnp.float32)
    inverse = jnp.exp(freq_steps * (-2.0 * math.log(10000.0) / HD))
    angles = positions.astype(jnp.float32)[:, None] * inverse[None, :]
    return (jnp.cos(angles), jnp.sin(angles))


def attention_kernel(
    start_ref, end_ref, cos_ref, sin_ref, q_ref, k_ref, vn_ref, kp_ref, vp_ref, o_ref
):
    score_scale = HD ** (-0.5)
    cosine = cos_ref[...]
    sine = sin_ref[...]

    def rotated(block):
        wide = block.astype(jnp.float32)
        swapped = pltpu.roll(wide, HD // 2, 1)
        return (wide * cosine + swapped * sine).astype(jnp.bfloat16)

    slots = q_ref.shape[0]
    rows = kp_ref.shape[0]
    places = lax.broadcasted_iota(jnp.int32, (slots, rows), 1)
    member = (places >= start_ref[...]) & (places < end_ref[...])
    for j in range(HEADS_PER_STEP):
        cols = slice(j * HD, (j + 1) * HD)
        query = rotated(q_ref[:, cols])
        key_rot = rotated(k_ref[:, cols])
        scores = (
            lax.dot_general(
                query,
                kp_ref[:, cols],
                (((1,), (1,)), ((), ())),
                preferred_element_type=jnp.float32,
            )
            * score_scale
        )
        own_score = (
            jnp.sum(
                query.astype(jnp.float32) * key_rot.astype(jnp.float32),
                axis=-1,
                keepdims=True,
            )
            * score_scale
        )
        masked = jnp.where(member, scores, -jnp.inf)
        row_top = jnp.maximum(jnp.max(masked, axis=-1, keepdims=True), own_score)
        weights = jnp.where(member, jnp.exp(scores - row_top), 0.0)
        own_weight = jnp.exp(own_score - row_top)
        row_total = jnp.sum(weights, axis=-1, keepdims=True) + own_weight
        summed = jnp.dot(
            weights.astype(jnp.bfloat16), vp_ref[:, cols], preferred_element_type=jnp.float32
        )
        own_bf = own_weight.astype(jnp.bfloat16).astype(jnp.float32)
        summed = summed + own_bf * vn_ref[:, cols].astype(jnp.float32)
        o_ref[:, cols] = (summed / row_total).astype(o_ref.dtype)


def attend_local(query_new, key_new, value_new, key_pool, value_pool, starts, ends, cos2, sin2):
    slots, width = query_new.shape
    rows = key_pool.shape[0]
    block = HEADS_PER_STEP * HD
    steps = width // block
    slot_spec = pl.BlockSpec((slots, block), lambda g: (0, g))
    pool_spec = pl.BlockSpec((rows, block), lambda g: (0, g))
    bound_spec = pl.BlockSpec((slots, 1), lambda g: (0, 0))
    table_spec = pl.BlockSpec((slots, HD), lambda g: (0, 0))
    flops = 4 * slots * rows * width
    return pl.pallas_call(
        attention_kernel,
        grid=(steps,),
        in_specs=[
            bound_spec,
            bound_spec,
            table_spec,
            table_spec,
            slot_spec,
            slot_spec,
            slot_spec,
            pool_spec,
            pool_spec,
        ],
        out_specs=slot_spec,
        out_shape=jax.ShapeDtypeStruct((slots, width), jnp.bfloat16),
        cost_estimate=pl.CostEstimate(
            flops=flops,
            transcendentals=slots * rows * (width // HD),
            bytes_accessed=2 * rows * width * 2 + 4 * slots * width * 2,
        ),
    )(starts, ends, cos2, sin2, query_new, key_new, value_new, key_pool, value_pool)


def gate_up_kernel(x_ref, w_ref, o_ref, acc, acc_sq):
    step = pl.program_id(0)
    quarters = x_ref.shape[1]
    width = x_ref.shape[3]
    columns = w_ref.shape[2]
    half = w_ref.shape[1] // 2
    units = o_ref.shape[0]

    @pl.when(step == 0)
    def _():
        acc[...] = jnp.zeros_like(acc)
        acc_sq[...] = jnp.zeros_like(acc_sq)

    def body(i, carry):
        weights = w_ref[i]
        for quarter in range(quarters):
            cols = slice(quarter * width, (quarter + 1) * width)
            block = x_ref[i, quarter, :columns, :]
            acc[:, cols] += jnp.dot(weights, block, preferred_element_type=jnp.float32)
            acc_sq[:, cols] += x_ref[i, quarter, columns:, :].astype(jnp.float32)
        return carry

    lax.fori_loop(0, x_ref.shape[0], body, 0)

    @pl.when(step == pl.num_programs(0) - 1)
    def _():
        squares = acc_sq[0:1, :] + acc_sq[1:2, :]
        inverse = lax.rsqrt(squares / D + 1e-05)
        gate_pre = acc[:half, :] * inverse
        silu = gate_pre / (1.0 + jnp.exp(-gate_pre))
        active = silu * (acc[half:, :] * inverse)
        o_ref[...] = active[:units].astype(o_ref.dtype)


def gate_up(hidden_t, weights_t, units):
    chunks, quarters, rows, width = hidden_t.shape
    both, columns = weights_t.shape[1], weights_t.shape[2]
    slots = quarters * width
    return pl.pallas_call(
        gate_up_kernel,
        grid=(chunks // R_PER_STEP,),
        in_specs=[
            pl.BlockSpec((R_PER_STEP, quarters, rows, width), lambda s: (s, 0, 0, 0)),
            pl.BlockSpec((R_PER_STEP, both, columns), lambda s: (s, 0, 0)),
        ],
        out_specs=pl.BlockSpec((units, slots), lambda s: (0, 0)),
        out_shape=jax.ShapeDtypeStruct((units, slots), jnp.bfloat16),
        scratch_shapes=[
            pltpu.VMEM((both, slots), jnp.float32),
            pltpu.VMEM((rows - columns, slots), jnp.float32),
        ],
        compiler_params=pltpu.CompilerParams(dimension_semantics=("arbitrary",)),
        cost_estimate=pl.CostEstimate(
            flops=2 * both * slots * chunks * columns,
            transcendentals=units * slots,
            bytes_accessed=hidden_t.size * 2 + weights_t.size * 2 + units * slots * 2,
        ),
    )(hidden_t, weights_t)


def body(
    query_new,
    key_new,
    value_new,
    key_pool,
    value_pool,
    lengths,
    slot_request,
    residual,
    out_proj,
    norm_gain,
    gate_proj,
    up_proj,
    down_proj,
):
    owned = query_new.shape[0]
    req_count = lax.axis_size(REQ)
    head_count = lax.axis_size(HEAD)
    first_slot = lax.axis_index(REQ) * owned
    my_requests = lax.dynamic_slice_in_dim(slot_request, first_slot, owned, 0)
    my_lengths = jnp.take(lengths, my_requests, axis=0)
    cosine, sine_table = rope_tables(my_lengths)
    cos2 = jnp.concatenate([cosine, cosine], axis=1)
    sin2 = jnp.concatenate([-sine_table, sine_table], axis=1)
    seg_ends = jnp.cumsum(my_lengths)
    starts = (seg_ends - my_lengths).astype(jnp.int32)
    attention = attend_local(
        query_new,
        key_new,
        value_new,
        key_pool,
        value_pool,
        starts[:, None],
        seg_ends.astype(jnp.int32)[:, None],
        cos2,
        sin2,
    )
    partial_sums = jnp.dot(
        lax.all_gather(attention, REQ, axis=0, tiled=True),
        out_proj,
        preferred_element_type=jnp.float32,
    )
    summed = lax.psum_scatter(partial_sums, HEAD, scatter_dimension=0, tiled=True)
    quarter = summed.shape[0]
    quarter_slots = lax.dynamic_slice_in_dim(
        slot_request, lax.axis_index(HEAD) * quarter, quarter, 0
    )
    attended = (jnp.take(residual, quarter_slots, axis=0).astype(jnp.float32) + summed).astype(
        jnp.bfloat16
    )
    column_width = attended.shape[1]
    widened = attended.astype(jnp.float32)
    partial_squares = jnp.sum(widened * widened, axis=1)
    high = partial_squares.astype(jnp.bfloat16)
    low = (partial_squares - high.astype(jnp.float32)).astype(jnp.bfloat16)
    pad_rows = SQ_ROWS - 2
    block_t = jnp.concatenate(
        [attended.T, high[None], low[None], jnp.zeros((pad_rows, quarter), jnp.bfloat16)], axis=0
    )
    hidden_t = lax.all_gather(block_t[None], REQ + (HEAD,), axis=0, tiled=True).reshape(
        req_count, head_count, column_width + SQ_ROWS, quarter
    )
    col_block = gate_proj.shape[1]
    gain = norm_gain.astype(jnp.float32)[:, None]
    padded = -(-col_block // 8) * 8

    def prepared(weights):
        scaled_w = (weights.astype(jnp.float32) * gain).astype(jnp.bfloat16)
        shaped_w = scaled_w.reshape(req_count, column_width, col_block).transpose(0, 2, 1)
        return jnp.pad(shaped_w, ((0, 0), (0, padded - col_block), (0, 0)))

    weights_t = jnp.concatenate([prepared(gate_proj), prepared(up_proj)], axis=1)
    active_t = gate_up(hidden_t, weights_t, col_block)
    active_all = lax.all_gather(active_t, HEAD, axis=0, tiled=True)
    down_sums = lax.dot_general(
        active_all, down_proj, (((0,), (0,)), ((), ())), preferred_element_type=jnp.float32
    )
    cores = lax.axis_size(CORE)
    chips = req_count // cores
    pieces = down_sums.astype(jnp.bfloat16).reshape(chips, cores, owned, down_sums.shape[1])
    my_core = lax.axis_index(CORE)
    kept = lax.dynamic_index_in_dim(pieces, my_core, axis=1, keepdims=False)
    sent = lax.dynamic_index_in_dim(pieces, cores - 1 - my_core, axis=1, keepdims=False)
    arrived = lax.ppermute(sent, CORE, [(core, cores - 1 - core) for core in range(cores)])
    chip_sums = (kept.astype(jnp.float32) + arrived.astype(jnp.float32)).astype(jnp.bfloat16)
    received = lax.all_to_all(chip_sums, CHIPS, 0, 0, tiled=True)
    ffn_out = jnp.sum(received.astype(jnp.float32), axis=0).astype(jnp.bfloat16)
    return (attended, ffn_out)


def solution(mesh):
    placed = (
        P(REQ, HEAD),
        P(REQ, HEAD),
        P(REQ, HEAD),
        P(REQ, HEAD),
        P(REQ, HEAD),
        P(),
        P(),
        P(None, REQ),
        P(HEAD, REQ),
        P(),
        P(None, REQ + (HEAD,)),
        P(None, REQ + (HEAD,)),
        P(REQ, HEAD),
    )
    req_size, head_size = mesh.devices.shape
    named = jax.sharding.Mesh(
        mesh.devices.reshape(req_size // CORES_PER_CHIP, CORES_PER_CHIP, head_size),
        (CHIPS, CORE, HEAD),
    )
    return jax.shard_map(
        body,
        mesh=named,
        in_specs=placed,
        out_specs=(P(HEAD, REQ), P(REQ, HEAD)),
        check_vma=False,
    )
```

```python
import math

import jax
import jax.numpy as jnp
from jax import lax
from jax.experimental import pallas as pl
from jax.experimental.pallas import tpu as pltpu
from jax.sharding import PartitionSpec as P

D = 5120
HD = 128
CHIPS = "chip"
CORE = "core"
REQ = (CHIPS, CORE)
CORES_PER_CHIP = 2
HEAD = "y"
HEADS_PER_STEP = 2
R_PER_STEP = 8
SQ_ROWS = 16


def rope_tables(positions):
    half_dim = HD // 2
    freq_steps = jnp.arange(half_dim, dtype=jnp.float32)
    inverse = jnp.exp(freq_steps * (-2.0 * math.log(10000.0) / HD))
    angles = positions.astype(jnp.float32)[:, None] * inverse[None, :]
    return (jnp.cos(angles), jnp.sin(angles))


def attention_kernel(
    start_ref, end_ref, cos_ref, sin_ref, q_ref, k_ref, vn_ref, kp_ref, vp_ref, o_ref
):
    score_scale = HD ** (-0.5)
    cosine = cos_ref[...]
    sine = sin_ref[...]

    def rotated(block):
        wide = block.astype(jnp.float32)
        swapped = pltpu.roll(wide, HD // 2, 1)
        return (wide * cosine + swapped * sine).astype(jnp.bfloat16)

    slots = q_ref.shape[0]
    rows = kp_ref.shape[0]
    places = lax.broadcasted_iota(jnp.int32, (slots, rows), 1)
    member = (places >= start_ref[...]) & (places < end_ref[...])
    for j in range(HEADS_PER_STEP):
        cols = slice(j * HD, (j + 1) * HD)
        query = rotated(q_ref[:, cols])
        key_rot = rotated(k_ref[:, cols])
        scores = (
            lax.dot_general(
                query,
                kp_ref[:, cols],
                (((1,), (1,)), ((), ())),
                preferred_element_type=jnp.float32,
            )
            * score_scale
        )
        own_score = (
            jnp.sum(
                query.astype(jnp.float32) * key_rot.astype(jnp.float32),
                axis=-1,
                keepdims=True,
            )
            * score_scale
        )
        masked = jnp.where(member, scores, -jnp.inf)
        row_top = jnp.maximum(jnp.max(masked, axis=-1, keepdims=True), own_score)
        weights = jnp.where(member, jnp.exp(scores - row_top), 0.0)
        own_weight = jnp.exp(own_score - row_top)
        row_total = jnp.sum(weights, axis=-1, keepdims=True) + own_weight
        summed = jnp.dot(
            weights.astype(jnp.bfloat16), vp_ref[:, cols], preferred_element_type=jnp.float32
        )
        own_bf = own_weight.astype(jnp.bfloat16).astype(jnp.float32)
        summed = summed + own_bf * vn_ref[:, cols].astype(jnp.float32)
        o_ref[:, cols] = (summed / row_total).astype(o_ref.dtype)


def attend_local(query_new, key_new, value_new, key_pool, value_pool, starts, ends, cos2, sin2):
    slots, width = query_new.shape
    rows = key_pool.shape[0]
    block = HEADS_PER_STEP * HD
    steps = width // block
    slot_spec = pl.BlockSpec((slots, block), lambda g: (0, g))
    pool_spec = pl.BlockSpec((rows, block), lambda g: (0, g))
    bound_spec = pl.BlockSpec((slots, 1), lambda g: (0, 0))
    table_spec = pl.BlockSpec((slots, HD), lambda g: (0, 0))
    flops = 4 * slots * rows * width
    return pl.pallas_call(
        attention_kernel,
        grid=(steps,),
        in_specs=[
            bound_spec,
            bound_spec,
            table_spec,
            table_spec,
            slot_spec,
            slot_spec,
            slot_spec,
            pool_spec,
            pool_spec,
        ],
        out_specs=slot_spec,
        out_shape=jax.ShapeDtypeStruct((slots, width), jnp.bfloat16),
        cost_estimate=pl.CostEstimate(
            flops=flops,
            transcendentals=slots * rows * (width // HD),
            bytes_accessed=2 * rows * width * 2 + 4 * slots * width * 2,
        ),
    )(starts, ends, cos2, sin2, query_new, key_new, value_new, key_pool, value_pool)


def gate_up_kernel(x_ref, w_ref, o_ref, acc, acc_sq):
    step = pl.program_id(0)
    quarters = x_ref.shape[1]
    width = x_ref.shape[3]
    columns = w_ref.shape[2]
    half = w_ref.shape[1] // 2
    units = o_ref.shape[0]

    @pl.when(step == 0)
    def _():
        acc[...] = jnp.zeros_like(acc)
        acc_sq[...] = jnp.zeros_like(acc_sq)

    def body(i, carry):
        weights = w_ref[i]
        for quarter in range(quarters):
            cols = slice(quarter * width, (quarter + 1) * width)
            block = x_ref[i, quarter, :columns, :]
            acc[:, cols] += jnp.dot(weights, block, preferred_element_type=jnp.float32)
            acc_sq[:, cols] += x_ref[i, quarter, columns:, :].astype(jnp.float32)
        return carry

    lax.fori_loop(0, x_ref.shape[0], body, 0)

    @pl.when(step == pl.num_programs(0) - 1)
    def _():
        squares = acc_sq[0:1, :] + acc_sq[1:2, :]
        inverse = lax.rsqrt(squares / D + 1e-05)
        gate_pre = acc[:half, :] * inverse
        silu = gate_pre / (1.0 + jnp.exp(-gate_pre))
        active = silu * (acc[half:, :] * inverse)
        o_ref[...] = active[:units].astype(o_ref.dtype)


def gate_up(hidden_t, weights_t, units):
    chunks, quarters, rows, width = hidden_t.shape
    both, columns = weights_t.shape[1], weights_t.shape[2]
    slots = quarters * width
    return pl.pallas_call(
        gate_up_kernel,
        grid=(chunks // R_PER_STEP,),
        in_specs=[
            pl.BlockSpec((R_PER_STEP, quarters, rows, width), lambda s: (s, 0, 0, 0)),
            pl.BlockSpec((R_PER_STEP, both, columns), lambda s: (s, 0, 0)),
        ],
        out_specs=pl.BlockSpec((units, slots), lambda s: (0, 0)),
        out_shape=jax.ShapeDtypeStruct((units, slots), jnp.bfloat16),
        scratch_shapes=[
            pltpu.VMEM((both, slots), jnp.float32),
            pltpu.VMEM((rows - columns, slots), jnp.float32),
        ],
        compiler_params=pltpu.CompilerParams(dimension_semantics=("arbitrary",)),
        cost_estimate=pl.CostEstimate(
            flops=2 * both * slots * chunks * columns,
            transcendentals=units * slots,
            bytes_accessed=hidden_t.size * 2 + weights_t.size * 2 + units * slots * 2,
        ),
    )(hidden_t, weights_t)


def body(
    query_new,
    key_new,
    value_new,
    key_pool,
    value_pool,
    lengths,
    slot_request,
    residual,
    out_proj,
    norm_gain,
    gate_proj,
    up_proj,
    down_proj,
):
    owned = query_new.shape[0]
    req_count = lax.axis_size(REQ)
    head_count = lax.axis_size(HEAD)
    first_slot = lax.axis_index(REQ) * owned
    my_requests = lax.dynamic_slice_in_dim(slot_request, first_slot, owned, 0)
    my_lengths = jnp.take(lengths, my_requests, axis=0)
    cosine, sine_table = rope_tables(my_lengths)
    cos2 = jnp.concatenate([cosine, cosine], axis=1)
    sin2 = jnp.concatenate([-sine_table, sine_table], axis=1)
    seg_ends = jnp.cumsum(my_lengths)
    starts = (seg_ends - my_lengths).astype(jnp.int32)
    attention = attend_local(
        query_new,
        key_new,
        value_new,
        key_pool,
        value_pool,
        starts[:, None],
        seg_ends.astype(jnp.int32)[:, None],
        cos2,
        sin2,
    )
    partial_sums = jnp.dot(
        lax.all_gather(attention, REQ, axis=0, tiled=True),
        out_proj,
        preferred_element_type=jnp.float32,
    )
    quarter = partial_sums.shape[0] // head_count
    exchanged = lax.all_to_all(
        partial_sums.reshape(head_count, quarter, partial_sums.shape[1]), HEAD, 0, 0, tiled=True
    )
    summed = jnp.sum(exchanged, axis=0)
    quarter_slots = lax.dynamic_slice_in_dim(
        slot_request, lax.axis_index(HEAD) * quarter, quarter, 0
    )
    attended = (jnp.take(residual, quarter_slots, axis=0).astype(jnp.float32) + summed).astype(
        jnp.bfloat16
    )
    column_width = attended.shape[1]
    widened = attended.astype(jnp.float32)
    partial_squares = jnp.sum(widened * widened, axis=1)
    high = partial_squares.astype(jnp.bfloat16)
    low = (partial_squares - high.astype(jnp.float32)).astype(jnp.bfloat16)
    pad_rows = SQ_ROWS - 2
    block_t = jnp.concatenate(
        [attended.T, high[None], low[None], jnp.zeros((pad_rows, quarter), jnp.bfloat16)], axis=0
    )
    hidden_t = lax.all_gather(block_t[None], REQ + (HEAD,), axis=0, tiled=True).reshape(
        req_count, head_count, column_width + SQ_ROWS, quarter
    )
    col_block = gate_proj.shape[1]
    gain = norm_gain.astype(jnp.float32)[:, None]
    padded = -(-col_block // 8) * 8

    def prepared(weights):
        scaled_w = (weights.astype(jnp.float32) * gain).astype(jnp.bfloat16)
        shaped_w = scaled_w.reshape(req_count, column_width, col_block).transpose(0, 2, 1)
        return jnp.pad(shaped_w, ((0, 0), (0, padded - col_block), (0, 0)))

    weights_t = jnp.concatenate([prepared(gate_proj), prepared(up_proj)], axis=1)
    active_t = gate_up(hidden_t, weights_t, col_block)
    active_all = lax.all_gather(active_t, HEAD, axis=0, tiled=True)
    down_sums = lax.dot_general(
        active_all, down_proj, (((0,), (0,)), ((), ())), preferred_element_type=jnp.float32
    )
    cores = lax.axis_size(CORE)
    chips = req_count // cores
    pieces = down_sums.astype(jnp.bfloat16).reshape(chips, cores, owned, down_sums.shape[1])
    my_core = lax.axis_index(CORE)
    kept = lax.dynamic_index_in_dim(pieces, my_core, axis=1, keepdims=False)
    sent = lax.dynamic_index_in_dim(pieces, cores - 1 - my_core, axis=1, keepdims=False)
    arrived = lax.ppermute(sent, CORE, [(core, cores - 1 - core) for core in range(cores)])
    chip_sums = (kept.astype(jnp.float32) + arrived.astype(jnp.float32)).astype(jnp.bfloat16)
    received = lax.all_to_all(chip_sums, CHIPS, 0, 0, tiled=True)
    ffn_out = jnp.sum(received.astype(jnp.float32), axis=0).astype(jnp.bfloat16)
    return (attended, ffn_out)


def solution(mesh):
    placed = (
        P(REQ, HEAD),
        P(REQ, HEAD),
        P(REQ, HEAD),
        P(REQ, HEAD),
        P(REQ, HEAD),
        P(),
        P(),
        P(None, REQ),
        P(HEAD, REQ),
        P(),
        P(None, REQ + (HEAD,)),
        P(None, REQ + (HEAD,)),
        P(REQ, HEAD),
    )
    req_size, head_size = mesh.devices.shape
    named = jax.sharding.Mesh(
        mesh.devices.reshape(req_size // CORES_PER_CHIP, CORES_PER_CHIP, head_size),
        (CHIPS, CORE, HEAD),
    )
    return jax.shard_map(
        body,
        mesh=named,
        in_specs=placed,
        out_specs=(P(HEAD, REQ), P(REQ, HEAD)),
        check_vma=False,
    )
```

```python
import math

import jax
import jax.numpy as jnp
from jax import lax
from jax.experimental import pallas as pl
from jax.experimental.pallas import tpu as pltpu
from jax.sharding import PartitionSpec as P

D = 5120
HD = 128
CHIPS = "chip"
CORE = "core"
REQ = (CHIPS, CORE)
CORES_PER_CHIP = 2
HEAD = "y"
HEADS_PER_STEP = 2
R_PER_STEP = 8
SQ_ROWS = 16


def rope_tables(positions):
    half_dim = HD // 2
    freq_steps = jnp.arange(half_dim, dtype=jnp.float32)
    inverse = jnp.exp(freq_steps * (-2.0 * math.log(10000.0) / HD))
    angles = positions.astype(jnp.float32)[:, None] * inverse[None, :]
    return (jnp.cos(angles), jnp.sin(angles))


def attention_kernel(
    start_ref, end_ref, cos_ref, sin_ref, q_ref, k_ref, vn_ref, kp_ref, vp_ref, o_ref
):
    score_scale = HD ** (-0.5)
    cosine = cos_ref[...]
    sine = sin_ref[...]

    def rotated(block):
        wide = block.astype(jnp.float32)
        swapped = pltpu.roll(wide, HD // 2, 1)
        return (wide * cosine + swapped * sine).astype(jnp.bfloat16)

    slots = q_ref.shape[0]
    rows = kp_ref.shape[0]
    places = lax.broadcasted_iota(jnp.int32, (slots, rows), 1)
    member = (places >= start_ref[...]) & (places < end_ref[...])
    for j in range(HEADS_PER_STEP):
        cols = slice(j * HD, (j + 1) * HD)
        query = rotated(q_ref[:, cols])
        key_rot = rotated(k_ref[:, cols])
        scores = (
            lax.dot_general(
                query,
                kp_ref[:, cols],
                (((1,), (1,)), ((), ())),
                preferred_element_type=jnp.float32,
            )
            * score_scale
        )
        own_score = (
            jnp.sum(
                query.astype(jnp.float32) * key_rot.astype(jnp.float32),
                axis=-1,
                keepdims=True,
            )
            * score_scale
        )
        masked = jnp.where(member, scores, -jnp.inf)
        row_top = jnp.maximum(jnp.max(masked, axis=-1, keepdims=True), own_score)
        weights = jnp.where(member, jnp.exp(scores - row_top), 0.0)
        own_weight = jnp.exp(own_score - row_top)
        row_total = jnp.sum(weights, axis=-1, keepdims=True) + own_weight
        summed = jnp.dot(
            weights.astype(jnp.bfloat16), vp_ref[:, cols], preferred_element_type=jnp.float32
        )
        own_bf = own_weight.astype(jnp.bfloat16).astype(jnp.float32)
        summed = summed + own_bf * vn_ref[:, cols].astype(jnp.float32)
        o_ref[:, cols] = (summed / row_total).astype(o_ref.dtype)


def attend_local(query_new, key_new, value_new, key_pool, value_pool, starts, ends, cos2, sin2):
    slots, width = query_new.shape
    rows = key_pool.shape[0]
    block = HEADS_PER_STEP * HD
    steps = width // block
    slot_spec = pl.BlockSpec((slots, block), lambda g: (0, g))
    pool_spec = pl.BlockSpec((rows, block), lambda g: (0, g))
    bound_spec = pl.BlockSpec((slots, 1), lambda g: (0, 0))
    table_spec = pl.BlockSpec((slots, HD), lambda g: (0, 0))
    flops = 4 * slots * rows * width
    return pl.pallas_call(
        attention_kernel,
        grid=(steps,),
        in_specs=[
            bound_spec,
            bound_spec,
            table_spec,
            table_spec,
            slot_spec,
            slot_spec,
            slot_spec,
            pool_spec,
            pool_spec,
        ],
        out_specs=slot_spec,
        out_shape=jax.ShapeDtypeStruct((slots, width), jnp.bfloat16),
        cost_estimate=pl.CostEstimate(
            flops=flops,
            transcendentals=slots * rows * (width // HD),
            bytes_accessed=2 * rows * width * 2 + 4 * slots * width * 2,
        ),
    )(starts, ends, cos2, sin2, query_new, key_new, value_new, key_pool, value_pool)


def gate_up_kernel(x_ref, w_ref, o_ref, acc, acc_sq):
    step = pl.program_id(0)
    quarters = x_ref.shape[1]
    width = x_ref.shape[3]
    columns = w_ref.shape[2]
    half = w_ref.shape[1] // 2
    units = o_ref.shape[0]

    @pl.when(step == 0)
    def _():
        acc[...] = jnp.zeros_like(acc)
        acc_sq[...] = jnp.zeros_like(acc_sq)

    def body(i, carry):
        weights = w_ref[i]
        for quarter in range(quarters):
            cols = slice(quarter * width, (quarter + 1) * width)
            block = x_ref[i, quarter, :columns, :]
            acc[:, cols] += jnp.dot(weights, block, preferred_element_type=jnp.float32)
            acc_sq[:, cols] += x_ref[i, quarter, columns:, :].astype(jnp.float32)
        return carry

    lax.fori_loop(0, x_ref.shape[0], body, 0)

    @pl.when(step == pl.num_programs(0) - 1)
    def _():
        squares = acc_sq[0:1, :] + acc_sq[1:2, :]
        inverse = lax.rsqrt(squares / D + 1e-05)
        gate_pre = acc[:half, :] * inverse
        silu = gate_pre / (1.0 + jnp.exp(-gate_pre))
        active = silu * (acc[half:, :] * inverse)
        o_ref[...] = active[:units].astype(o_ref.dtype)


def gate_up(hidden_t, weights_t, units):
    chunks, quarters, rows, width = hidden_t.shape
    both, columns = weights_t.shape[1], weights_t.shape[2]
    slots = quarters * width
    return pl.pallas_call(
        gate_up_kernel,
        grid=(chunks // R_PER_STEP,),
        in_specs=[
            pl.BlockSpec((R_PER_STEP, quarters, rows, width), lambda s: (s, 0, 0, 0)),
            pl.BlockSpec((R_PER_STEP, both, columns), lambda s: (s, 0, 0)),
        ],
        out_specs=pl.BlockSpec((units, slots), lambda s: (0, 0)),
        out_shape=jax.ShapeDtypeStruct((units, slots), jnp.bfloat16),
        scratch_shapes=[
            pltpu.VMEM((both, slots), jnp.float32),
            pltpu.VMEM((rows - columns, slots), jnp.float32),
        ],
        compiler_params=pltpu.CompilerParams(dimension_semantics=("arbitrary",)),
        cost_estimate=pl.CostEstimate(
            flops=2 * both * slots * chunks * columns,
            transcendentals=units * slots,
            bytes_accessed=hidden_t.size * 2 + weights_t.size * 2 + units * slots * 2,
        ),
    )(hidden_t, weights_t)


def body(
    query_new,
    key_new,
    value_new,
    key_pool,
    value_pool,
    lengths,
    slot_request,
    residual,
    out_proj,
    norm_gain,
    gate_proj,
    up_proj,
    down_proj,
):
    owned = query_new.shape[0]
    req_count = lax.axis_size(REQ)
    head_count = lax.axis_size(HEAD)
    first_slot = lax.axis_index(REQ) * owned
    my_requests = lax.dynamic_slice_in_dim(slot_request, first_slot, owned, 0)
    my_lengths = jnp.take(lengths, my_requests, axis=0)
    cosine, sine_table = rope_tables(my_lengths)
    cos2 = jnp.concatenate([cosine, cosine], axis=1)
    sin2 = jnp.concatenate([-sine_table, sine_table], axis=1)
    seg_ends = jnp.cumsum(my_lengths)
    starts = (seg_ends - my_lengths).astype(jnp.int32)
    attention = attend_local(
        query_new,
        key_new,
        value_new,
        key_pool,
        value_pool,
        starts[:, None],
        seg_ends.astype(jnp.int32)[:, None],
        cos2,
        sin2,
    )
    partial_sums = jnp.dot(
        lax.all_gather(attention, REQ, axis=0, tiled=True),
        out_proj,
        preferred_element_type=jnp.float32,
    )
    summed = lax.psum_scatter(partial_sums, HEAD, scatter_dimension=0, tiled=True)
    quarter = summed.shape[0]
    quarter_slots = lax.dynamic_slice_in_dim(
        slot_request, lax.axis_index(HEAD) * quarter, quarter, 0
    )
    attended = (jnp.take(residual, quarter_slots, axis=0).astype(jnp.float32) + summed).astype(
        jnp.bfloat16
    )
    column_width = attended.shape[1]
    widened = attended.astype(jnp.float32)
    partial_squares = jnp.sum(widened * widened, axis=1)
    high = partial_squares.astype(jnp.bfloat16)
    low = (partial_squares - high.astype(jnp.float32)).astype(jnp.bfloat16)
    pad_rows = SQ_ROWS - 2
    block_t = jnp.concatenate(
        [attended.T, high[None], low[None], jnp.zeros((pad_rows, quarter), jnp.bfloat16)], axis=0
    )
    hidden_t = lax.all_gather(block_t[None], REQ + (HEAD,), axis=0, tiled=True).reshape(
        req_count, head_count, column_width + SQ_ROWS, quarter
    )
    col_block = gate_proj.shape[1]
    gain = norm_gain.astype(jnp.float32)[:, None]
    padded = -(-col_block // 8) * 8

    def prepared(weights):
        scaled_w = (weights.astype(jnp.float32) * gain).astype(jnp.bfloat16)
        shaped_w = scaled_w.reshape(req_count, column_width, col_block).transpose(0, 2, 1)
        return jnp.pad(shaped_w, ((0, 0), (0, padded - col_block), (0, 0)))

    weights_t = jnp.concatenate([prepared(gate_proj), prepared(up_proj)], axis=1)
    active_t = gate_up(hidden_t, weights_t, col_block)
    active_all = lax.all_gather(active_t, HEAD, axis=0, tiled=True)
    cores = lax.axis_size(CORE)
    chips = req_count // cores
    units_all = active_all.shape[0]
    by_core = active_all.reshape(units_all, chips, cores, owned)
    my_core = lax.axis_index(CORE)

    def down_for(core):
        columns = lax.dynamic_index_in_dim(by_core, core, axis=2, keepdims=False)
        sums = lax.dot_general(
            columns.reshape(units_all, chips * owned),
            down_proj,
            (((0,), (0,)), ((), ())),
            preferred_element_type=jnp.float32,
        )
        return sums.astype(jnp.bfloat16).reshape(chips, owned, sums.shape[1])

    sent = down_for(cores - 1 - my_core)
    arrived = lax.ppermute(sent, CORE, [(core, cores - 1 - core) for core in range(cores)])
    kept = down_for(my_core)
    chip_sums = (kept.astype(jnp.float32) + arrived.astype(jnp.float32)).astype(jnp.bfloat16)
    received = lax.all_to_all(chip_sums, CHIPS, 0, 0, tiled=True)
    ffn_out = jnp.sum(received.astype(jnp.float32), axis=0).astype(jnp.bfloat16)
    return (attended, ffn_out)


def solution(mesh):
    placed = (
        P(REQ, HEAD),
        P(REQ, HEAD),
        P(REQ, HEAD),
        P(REQ, HEAD),
        P(REQ, HEAD),
        P(),
        P(),
        P(None, REQ),
        P(HEAD, REQ),
        P(),
        P(None, REQ + (HEAD,)),
        P(None, REQ + (HEAD,)),
        P(REQ, HEAD),
    )
    req_size, head_size = mesh.devices.shape
    named = jax.sharding.Mesh(
        mesh.devices.reshape(req_size // CORES_PER_CHIP, CORES_PER_CHIP, head_size),
        (CHIPS, CORE, HEAD),
    )
    return jax.shard_map(
        body,
        mesh=named,
        in_specs=placed,
        out_specs=(P(HEAD, REQ), P(REQ, HEAD)),
        check_vma=False,
    )
```

```python
import math

import jax
import jax.numpy as jnp
from jax import lax
from jax.experimental import pallas as pl
from jax.experimental.pallas import tpu as pltpu
from jax.sharding import PartitionSpec as P

D = 5120
HD = 128
CHIPS = "chip"
CORE = "core"
REQ = (CHIPS, CORE)
CORES_PER_CHIP = 2
HEAD = "y"
HEADS_PER_STEP = 2
R_PER_STEP = 8
SQ_ROWS = 16


def rope_tables(positions):
    half_dim = HD // 2
    freq_steps = jnp.arange(half_dim, dtype=jnp.float32)
    inverse = jnp.exp(freq_steps * (-2.0 * math.log(10000.0) / HD))
    angles = positions.astype(jnp.float32)[:, None] * inverse[None, :]
    return (jnp.cos(angles), jnp.sin(angles))


def attention_kernel(
    start_ref, end_ref, cos_ref, sin_ref, q_ref, k_ref, vn_ref, kp_ref, vp_ref, o_ref
):
    score_scale = HD ** (-0.5)
    cosine = cos_ref[...]
    sine = sin_ref[...]

    def rotated(block):
        wide = block.astype(jnp.float32)
        swapped = pltpu.roll(wide, HD // 2, 1)
        return (wide * cosine + swapped * sine).astype(jnp.bfloat16)

    slots = q_ref.shape[0]
    rows = kp_ref.shape[0]
    places = lax.broadcasted_iota(jnp.int32, (slots, rows), 1)
    member = (places >= start_ref[...]) & (places < end_ref[...])
    for j in range(HEADS_PER_STEP):
        cols = slice(j * HD, (j + 1) * HD)
        query = rotated(q_ref[:, cols])
        key_rot = rotated(k_ref[:, cols])
        scores = (
            lax.dot_general(
                query,
                kp_ref[:, cols],
                (((1,), (1,)), ((), ())),
                preferred_element_type=jnp.float32,
            )
            * score_scale
        )
        own_score = (
            jnp.sum(
                query.astype(jnp.float32) * key_rot.astype(jnp.float32),
                axis=-1,
                keepdims=True,
            )
            * score_scale
        )
        masked = jnp.where(member, scores, -jnp.inf)
        row_top = jnp.maximum(jnp.max(masked, axis=-1, keepdims=True), own_score)
        weights = jnp.where(member, jnp.exp(scores - row_top), 0.0)
        own_weight = jnp.exp(own_score - row_top)
        row_total = jnp.sum(weights, axis=-1, keepdims=True) + own_weight
        summed = jnp.dot(
            weights.astype(jnp.bfloat16), vp_ref[:, cols], preferred_element_type=jnp.float32
        )
        own_bf = own_weight.astype(jnp.bfloat16).astype(jnp.float32)
        summed = summed + own_bf * vn_ref[:, cols].astype(jnp.float32)
        o_ref[:, cols] = (summed / row_total).astype(o_ref.dtype)


def attend_local(query_new, key_new, value_new, key_pool, value_pool, starts, ends, cos2, sin2):
    slots, width = query_new.shape
    rows = key_pool.shape[0]
    block = HEADS_PER_STEP * HD
    steps = width // block
    slot_spec = pl.BlockSpec((slots, block), lambda g: (0, g))
    pool_spec = pl.BlockSpec((rows, block), lambda g: (0, g))
    bound_spec = pl.BlockSpec((slots, 1), lambda g: (0, 0))
    table_spec = pl.BlockSpec((slots, HD), lambda g: (0, 0))
    flops = 4 * slots * rows * width
    return pl.pallas_call(
        attention_kernel,
        grid=(steps,),
        in_specs=[
            bound_spec,
            bound_spec,
            table_spec,
            table_spec,
            slot_spec,
            slot_spec,
            slot_spec,
            pool_spec,
            pool_spec,
        ],
        out_specs=slot_spec,
        out_shape=jax.ShapeDtypeStruct((slots, width), jnp.bfloat16),
        cost_estimate=pl.CostEstimate(
            flops=flops,
            transcendentals=slots * rows * (width // HD),
            bytes_accessed=2 * rows * width * 2 + 4 * slots * width * 2,
        ),
    )(starts, ends, cos2, sin2, query_new, key_new, value_new, key_pool, value_pool)


def gate_up_kernel(x_ref, w_ref, o_ref, acc, acc_sq):
    step = pl.program_id(0)
    quarters = x_ref.shape[1]
    width = x_ref.shape[3]
    columns = w_ref.shape[2]
    half = w_ref.shape[1] // 2
    units = o_ref.shape[0]

    @pl.when(step == 0)
    def _():
        acc[...] = jnp.zeros_like(acc)
        acc_sq[...] = jnp.zeros_like(acc_sq)

    def body(i, carry):
        weights = w_ref[i]
        for quarter in range(quarters):
            cols = slice(quarter * width, (quarter + 1) * width)
            block = x_ref[i, quarter, :columns, :]
            acc[:, cols] += jnp.dot(weights, block, preferred_element_type=jnp.float32)
            acc_sq[:, cols] += x_ref[i, quarter, columns:, :].astype(jnp.float32)
        return carry

    lax.fori_loop(0, x_ref.shape[0], body, 0)

    @pl.when(step == pl.num_programs(0) - 1)
    def _():
        squares = acc_sq[0:1, :] + acc_sq[1:2, :]
        inverse = lax.rsqrt(squares / D + 1e-05)
        gate_pre = acc[:half, :] * inverse
        silu = gate_pre / (1.0 + jnp.exp(-gate_pre))
        active = silu * (acc[half:, :] * inverse)
        o_ref[...] = active[:units].astype(o_ref.dtype)


def gate_up(hidden_t, weights_t, units):
    chunks, quarters, rows, width = hidden_t.shape
    both, columns = weights_t.shape[1], weights_t.shape[2]
    slots = quarters * width
    return pl.pallas_call(
        gate_up_kernel,
        grid=(chunks // R_PER_STEP,),
        in_specs=[
            pl.BlockSpec((R_PER_STEP, quarters, rows, width), lambda s: (s, 0, 0, 0)),
            pl.BlockSpec((R_PER_STEP, both, columns), lambda s: (s, 0, 0)),
        ],
        out_specs=pl.BlockSpec((units, slots), lambda s: (0, 0)),
        out_shape=jax.ShapeDtypeStruct((units, slots), jnp.bfloat16),
        scratch_shapes=[
            pltpu.VMEM((both, slots), jnp.float32),
            pltpu.VMEM((rows - columns, slots), jnp.float32),
        ],
        compiler_params=pltpu.CompilerParams(dimension_semantics=("arbitrary",)),
        cost_estimate=pl.CostEstimate(
            flops=2 * both * slots * chunks * columns,
            transcendentals=units * slots,
            bytes_accessed=hidden_t.size * 2 + weights_t.size * 2 + units * slots * 2,
        ),
    )(hidden_t, weights_t)


def body(
    query_new,
    key_new,
    value_new,
    key_pool,
    value_pool,
    lengths,
    slot_request,
    residual,
    out_proj,
    norm_gain,
    gate_proj,
    up_proj,
    down_proj,
):
    owned = query_new.shape[0]
    req_count = lax.axis_size(REQ)
    head_count = lax.axis_size(HEAD)
    first_slot = lax.axis_index(REQ) * owned
    my_requests = lax.dynamic_slice_in_dim(slot_request, first_slot, owned, 0)
    my_lengths = jnp.take(lengths, my_requests, axis=0)
    cosine, sine_table = rope_tables(my_lengths)
    cos2 = jnp.concatenate([cosine, cosine], axis=1)
    sin2 = jnp.concatenate([-sine_table, sine_table], axis=1)
    seg_ends = jnp.cumsum(my_lengths)
    starts = (seg_ends - my_lengths).astype(jnp.int32)
    attention = attend_local(
        query_new,
        key_new,
        value_new,
        key_pool,
        value_pool,
        starts[:, None],
        seg_ends.astype(jnp.int32)[:, None],
        cos2,
        sin2,
    )
    partial_sums = jnp.dot(
        lax.all_gather(attention, REQ, axis=0, tiled=True),
        out_proj,
        preferred_element_type=jnp.float32,
    )
    summed = lax.psum_scatter(partial_sums, HEAD, scatter_dimension=0, tiled=True)
    quarter = summed.shape[0]
    quarter_slots = lax.dynamic_slice_in_dim(
        slot_request, lax.axis_index(HEAD) * quarter, quarter, 0
    )
    attended = (jnp.take(residual, quarter_slots, axis=0).astype(jnp.float32) + summed).astype(
        jnp.bfloat16
    )
    column_width = attended.shape[1]
    widened = attended.astype(jnp.float32)
    partial_squares = jnp.sum(widened * widened, axis=1)
    high = partial_squares.astype(jnp.bfloat16)
    low = (partial_squares - high.astype(jnp.float32)).astype(jnp.bfloat16)
    pad_rows = SQ_ROWS - 2
    block_t = jnp.concatenate(
        [attended.T, high[None], low[None], jnp.zeros((pad_rows, quarter), jnp.bfloat16)], axis=0
    )
    cores = lax.axis_size(CORE)
    owner_pairs = quarter // (owned * cores)
    block_t = (
        block_t.reshape(block_t.shape[0], owner_pairs, cores, owned)
        .transpose(0, 2, 1, 3)
        .reshape(block_t.shape[0], quarter)
    )
    hidden_t = lax.all_gather(block_t[None], REQ + (HEAD,), axis=0, tiled=True).reshape(
        req_count, head_count, column_width + SQ_ROWS, quarter
    )
    col_block = gate_proj.shape[1]
    gain = norm_gain.astype(jnp.float32)[:, None]
    padded = -(-col_block // 8) * 8

    def prepared(weights):
        scaled_w = (weights.astype(jnp.float32) * gain).astype(jnp.bfloat16)
        shaped_w = scaled_w.reshape(req_count, column_width, col_block).transpose(0, 2, 1)
        return jnp.pad(shaped_w, ((0, 0), (0, padded - col_block), (0, 0)))

    weights_t = jnp.concatenate([prepared(gate_proj), prepared(up_proj)], axis=1)
    active_t = gate_up(hidden_t, weights_t, col_block)
    active_all = lax.all_gather(active_t, HEAD, axis=0, tiled=True)
    chips = req_count // cores
    units_all = active_all.shape[0]
    by_core = active_all.reshape(units_all, head_count, cores, owner_pairs * owned)
    my_core = lax.axis_index(CORE)

    def down_for(core):
        columns = lax.dynamic_index_in_dim(by_core, core, axis=2, keepdims=False)
        sums = lax.dot_general(
            columns.reshape(units_all, chips * owned),
            down_proj,
            (((0,), (0,)), ((), ())),
            preferred_element_type=jnp.float32,
        )
        return sums.astype(jnp.bfloat16).reshape(chips, owned, sums.shape[1])

    sent = down_for(cores - 1 - my_core)
    arrived = lax.ppermute(sent, CORE, [(core, cores - 1 - core) for core in range(cores)])
    kept = down_for(my_core)
    chip_sums = (kept.astype(jnp.float32) + arrived.astype(jnp.float32)).astype(jnp.bfloat16)
    received = lax.all_to_all(chip_sums, CHIPS, 0, 0, tiled=True)
    ffn_out = jnp.sum(received.astype(jnp.float32), axis=0).astype(jnp.bfloat16)
    return (attended, ffn_out)


def solution(mesh):
    placed = (
        P(REQ, HEAD),
        P(REQ, HEAD),
        P(REQ, HEAD),
        P(REQ, HEAD),
        P(REQ, HEAD),
        P(),
        P(),
        P(None, REQ),
        P(HEAD, REQ),
        P(),
        P(None, REQ + (HEAD,)),
        P(None, REQ + (HEAD,)),
        P(REQ, HEAD),
    )
    req_size, head_size = mesh.devices.shape
    named = jax.sharding.Mesh(
        mesh.devices.reshape(req_size // CORES_PER_CHIP, CORES_PER_CHIP, head_size),
        (CHIPS, CORE, HEAD),
    )
    return jax.shard_map(
        body,
        mesh=named,
        in_specs=placed,
        out_specs=(P(HEAD, REQ), P(REQ, HEAD)),
        check_vma=False,
    )
```

```python
import math

import jax
import jax.numpy as jnp
from jax import lax
from jax.experimental import pallas as pl
from jax.experimental.pallas import tpu as pltpu
from jax.sharding import PartitionSpec as P

D = 5120
HD = 128
CHIPS = "chip"
CORE = "core"
REQ = (CHIPS, CORE)
CORES_PER_CHIP = 2
HEAD = "y"
HEADS_PER_STEP = 2
R_PER_STEP = 8
SQ_ROWS = 16


def rope_tables(positions):
    half_dim = HD // 2
    freq_steps = jnp.arange(half_dim, dtype=jnp.float32)
    inverse = jnp.exp(freq_steps * (-2.0 * math.log(10000.0) / HD))
    angles = positions.astype(jnp.float32)[:, None] * inverse[None, :]
    return (jnp.cos(angles), jnp.sin(angles))


def attention_kernel(
    start_ref, end_ref, cos_ref, sin_ref, q_ref, k_ref, vn_ref, kp_ref, vp_ref, o_ref
):
    score_scale = HD ** (-0.5)
    cosine = cos_ref[...]
    sine = sin_ref[...]

    def rotated(block):
        wide = block.astype(jnp.float32)
        swapped = pltpu.roll(wide, HD // 2, 1)
        return (wide * cosine + swapped * sine).astype(jnp.bfloat16)

    slots = q_ref.shape[0]
    rows = kp_ref.shape[0]
    places = lax.broadcasted_iota(jnp.int32, (slots, rows), 1)
    member = (places >= start_ref[...]) & (places < end_ref[...])
    for j in range(HEADS_PER_STEP):
        cols = slice(j * HD, (j + 1) * HD)
        query = rotated(q_ref[:, cols])
        key_rot = rotated(k_ref[:, cols])
        scores = (
            lax.dot_general(
                query,
                kp_ref[:, cols],
                (((1,), (1,)), ((), ())),
                preferred_element_type=jnp.float32,
            )
            * score_scale
        )
        own_score = (
            jnp.sum(
                query.astype(jnp.float32) * key_rot.astype(jnp.float32),
                axis=-1,
                keepdims=True,
            )
            * score_scale
        )
        masked = jnp.where(member, scores, -jnp.inf)
        row_top = jnp.maximum(jnp.max(masked, axis=-1, keepdims=True), own_score)
        weights = jnp.where(member, jnp.exp(scores - row_top), 0.0)
        own_weight = jnp.exp(own_score - row_top)
        row_total = jnp.sum(weights, axis=-1, keepdims=True) + own_weight
        summed = jnp.dot(
            weights.astype(jnp.bfloat16), vp_ref[:, cols], preferred_element_type=jnp.float32
        )
        own_bf = own_weight.astype(jnp.bfloat16).astype(jnp.float32)
        summed = summed + own_bf * vn_ref[:, cols].astype(jnp.float32)
        o_ref[:, cols] = (summed / row_total).astype(o_ref.dtype)


def attend_local(query_new, key_new, value_new, key_pool, value_pool, starts, ends, cos2, sin2):
    slots, width = query_new.shape
    rows = key_pool.shape[0]
    block = HEADS_PER_STEP * HD
    steps = width // block
    slot_spec = pl.BlockSpec((slots, block), lambda g: (0, g))
    pool_spec = pl.BlockSpec((rows, block), lambda g: (0, g))
    bound_spec = pl.BlockSpec((slots, 1), lambda g: (0, 0))
    table_spec = pl.BlockSpec((slots, HD), lambda g: (0, 0))
    flops = 4 * slots * rows * width
    return pl.pallas_call(
        attention_kernel,
        grid=(steps,),
        in_specs=[
            bound_spec,
            bound_spec,
            table_spec,
            table_spec,
            slot_spec,
            slot_spec,
            slot_spec,
            pool_spec,
            pool_spec,
        ],
        out_specs=slot_spec,
        out_shape=jax.ShapeDtypeStruct((slots, width), jnp.bfloat16),
        cost_estimate=pl.CostEstimate(
            flops=flops,
            transcendentals=slots * rows * (width // HD),
            bytes_accessed=2 * rows * width * 2 + 4 * slots * width * 2,
        ),
    )(starts, ends, cos2, sin2, query_new, key_new, value_new, key_pool, value_pool)


def gate_up_kernel(x_ref, w_ref, o_ref, acc, acc_sq):
    step = pl.program_id(0)
    quarters = x_ref.shape[1]
    width = x_ref.shape[3]
    columns = w_ref.shape[2]
    half = w_ref.shape[1] // 2
    units = o_ref.shape[0]

    @pl.when(step == 0)
    def _():
        acc[...] = jnp.zeros_like(acc)
        acc_sq[...] = jnp.zeros_like(acc_sq)

    def body(i, carry):
        weights = w_ref[i]
        for quarter in range(quarters):
            cols = slice(quarter * width, (quarter + 1) * width)
            block = x_ref[i, quarter, :columns, :]
            acc[:, cols] += jnp.dot(weights, block, preferred_element_type=jnp.float32)
            acc_sq[:, cols] += x_ref[i, quarter, columns:, :].astype(jnp.float32)
        return carry

    lax.fori_loop(0, x_ref.shape[0], body, 0)

    @pl.when(step == pl.num_programs(0) - 1)
    def _():
        squares = acc_sq[0:1, :] + acc_sq[1:2, :]
        inverse = lax.rsqrt(squares / D + 1e-05)
        gate_pre = acc[:half, :] * inverse
        silu = gate_pre / (1.0 + jnp.exp(-gate_pre))
        active = silu * (acc[half:, :] * inverse)
        o_ref[...] = active[:units].astype(o_ref.dtype)


def gate_up(hidden_t, weights_t, units):
    chunks, quarters, rows, width = hidden_t.shape
    both, columns = weights_t.shape[1], weights_t.shape[2]
    slots = quarters * width
    return pl.pallas_call(
        gate_up_kernel,
        grid=(chunks // R_PER_STEP,),
        in_specs=[
            pl.BlockSpec((R_PER_STEP, quarters, rows, width), lambda s: (s, 0, 0, 0)),
            pl.BlockSpec((R_PER_STEP, both, columns), lambda s: (s, 0, 0)),
        ],
        out_specs=pl.BlockSpec((units, slots), lambda s: (0, 0)),
        out_shape=jax.ShapeDtypeStruct((units, slots), jnp.bfloat16),
        scratch_shapes=[
            pltpu.VMEM((both, slots), jnp.float32),
            pltpu.VMEM((rows - columns, slots), jnp.float32),
        ],
        compiler_params=pltpu.CompilerParams(dimension_semantics=("arbitrary",)),
        cost_estimate=pl.CostEstimate(
            flops=2 * both * slots * chunks * columns,
            transcendentals=units * slots,
            bytes_accessed=hidden_t.size * 2 + weights_t.size * 2 + units * slots * 2,
        ),
    )(hidden_t, weights_t)


def body(
    query_new,
    key_new,
    value_new,
    key_pool,
    value_pool,
    lengths,
    slot_request,
    residual,
    out_proj,
    norm_gain,
    gate_proj,
    up_proj,
    down_proj,
):
    owned = query_new.shape[0]
    req_count = lax.axis_size(REQ)
    head_count = lax.axis_size(HEAD)
    first_slot = lax.axis_index(REQ) * owned
    my_requests = lax.dynamic_slice_in_dim(slot_request, first_slot, owned, 0)
    my_lengths = jnp.take(lengths, my_requests, axis=0)
    cosine, sine_table = rope_tables(my_lengths)
    cos2 = jnp.concatenate([cosine, cosine], axis=1)
    sin2 = jnp.concatenate([-sine_table, sine_table], axis=1)
    seg_ends = jnp.cumsum(my_lengths)
    starts = (seg_ends - my_lengths).astype(jnp.int32)
    attention = attend_local(
        query_new,
        key_new,
        value_new,
        key_pool,
        value_pool,
        starts[:, None],
        seg_ends.astype(jnp.int32)[:, None],
        cos2,
        sin2,
    )
    partial_sums = jnp.dot(
        lax.all_gather(attention, REQ, axis=0, tiled=True),
        out_proj,
        preferred_element_type=jnp.float32,
    )
    summed = lax.psum_scatter(partial_sums, HEAD, scatter_dimension=0, tiled=True)
    quarter = summed.shape[0]
    quarter_slots = lax.dynamic_slice_in_dim(
        slot_request, lax.axis_index(HEAD) * quarter, quarter, 0
    )
    attended = (jnp.take(residual, quarter_slots, axis=0).astype(jnp.float32) + summed).astype(
        jnp.bfloat16
    )
    column_width = attended.shape[1]
    widened = attended.astype(jnp.float32)
    partial_squares = jnp.sum(widened * widened, axis=1)
    high = partial_squares.astype(jnp.bfloat16)
    low = (partial_squares - high.astype(jnp.float32)).astype(jnp.bfloat16)
    pad_rows = SQ_ROWS - 2
    block_t = jnp.concatenate(
        [attended.T, high[None], low[None], jnp.zeros((pad_rows, quarter), jnp.bfloat16)], axis=0
    )
    hidden_t = lax.all_gather(block_t[None], REQ + (HEAD,), axis=0, tiled=True).reshape(
        req_count, head_count, column_width + SQ_ROWS, quarter
    )
    col_block = gate_proj.shape[1]
    gain = norm_gain.astype(jnp.float32)[:, None]
    padded = -(-col_block // 8) * 8

    def prepared(weights):
        scaled_w = (weights.astype(jnp.float32) * gain).astype(jnp.bfloat16)
        shaped_w = scaled_w.reshape(req_count, column_width, col_block).transpose(0, 2, 1)
        return jnp.pad(shaped_w, ((0, 0), (0, padded - col_block), (0, 0)))

    weights_t = jnp.concatenate([prepared(gate_proj), prepared(up_proj)], axis=1)
    active_t = gate_up(hidden_t, weights_t, col_block)
    active_all = lax.all_gather(active_t, HEAD, axis=0, tiled=True)
    cores = lax.axis_size(CORE)
    chips = req_count // cores
    units_all = active_all.shape[0]
    by_core = active_all.reshape(units_all, chips, cores, owned)
    my_core = lax.axis_index(CORE)

    def down_for(core):
        columns = by_core[:, :, core, :]
        sums = lax.dot_general(
            columns.reshape(units_all, chips * owned),
            down_proj,
            (((0,), (0,)), ((), ())),
            preferred_element_type=jnp.float32,
        )
        return sums.astype(jnp.bfloat16).reshape(chips, owned, sums.shape[1])

    halves = [down_for(core) for core in range(cores)]
    first_core = my_core == 0
    sent = jnp.where(first_core, halves[1], halves[0])
    arrived = lax.ppermute(sent, CORE, [(core, cores - 1 - core) for core in range(cores)])
    kept = jnp.where(first_core, halves[0], halves[1])
    chip_sums = (kept.astype(jnp.float32) + arrived.astype(jnp.float32)).astype(jnp.bfloat16)
    received = lax.all_to_all(chip_sums, CHIPS, 0, 0, tiled=True)
    ffn_out = jnp.sum(received.astype(jnp.float32), axis=0).astype(jnp.bfloat16)
    return (attended, ffn_out)


def solution(mesh):
    placed = (
        P(REQ, HEAD),
        P(REQ, HEAD),
        P(REQ, HEAD),
        P(REQ, HEAD),
        P(REQ, HEAD),
        P(),
        P(),
        P(None, REQ),
        P(HEAD, REQ),
        P(),
        P(None, REQ + (HEAD,)),
        P(None, REQ + (HEAD,)),
        P(REQ, HEAD),
    )
    req_size, head_size = mesh.devices.shape
    named = jax.sharding.Mesh(
        mesh.devices.reshape(req_size // CORES_PER_CHIP, CORES_PER_CHIP, head_size),
        (CHIPS, CORE, HEAD),
    )
    return jax.shard_map(
        body,
        mesh=named,
        in_specs=placed,
        out_specs=(P(HEAD, REQ), P(REQ, HEAD)),
        check_vma=False,
    )
```

```python
import math

import jax
import jax.numpy as jnp
from jax import lax
from jax.experimental import pallas as pl
from jax.experimental.pallas import tpu as pltpu
from jax.sharding import PartitionSpec as P

D = 5120
HD = 128
CHIPS = "chip"
CORE = "core"
REQ = (CHIPS, CORE)
CORES_PER_CHIP = 2
HEAD = "y"
HEADS_PER_STEP = 2
R_PER_STEP = 8
SQ_ROWS = 16


def rope_tables(positions):
    half_dim = HD // 2
    freq_steps = jnp.arange(half_dim, dtype=jnp.float32)
    inverse = jnp.exp(freq_steps * (-2.0 * math.log(10000.0) / HD))
    angles = positions.astype(jnp.float32)[:, None] * inverse[None, :]
    return (jnp.cos(angles), jnp.sin(angles))


def attention_kernel(
    start_ref, end_ref, cos_ref, sin_ref, q_ref, k_ref, vn_ref, kp_ref, vp_ref, o_ref
):
    score_scale = HD ** (-0.5)
    cosine = cos_ref[...]
    sine = sin_ref[...]

    def rotated(block):
        wide = block.astype(jnp.float32)
        swapped = pltpu.roll(wide, HD // 2, 1)
        return (wide * cosine + swapped * sine).astype(jnp.bfloat16)

    slots = q_ref.shape[0]
    rows = kp_ref.shape[0]
    places = lax.broadcasted_iota(jnp.int32, (slots, rows), 1)
    member = (places >= start_ref[...]) & (places < end_ref[...])
    for j in range(HEADS_PER_STEP):
        cols = slice(j * HD, (j + 1) * HD)
        query = rotated(q_ref[:, cols])
        key_rot = rotated(k_ref[:, cols])
        scores = (
            lax.dot_general(
                query,
                kp_ref[:, cols],
                (((1,), (1,)), ((), ())),
                preferred_element_type=jnp.float32,
            )
            * score_scale
        )
        own_score = (
            jnp.sum(
                query.astype(jnp.float32) * key_rot.astype(jnp.float32),
                axis=-1,
                keepdims=True,
            )
            * score_scale
        )
        masked = jnp.where(member, scores, -jnp.inf)
        row_top = jnp.maximum(jnp.max(masked, axis=-1, keepdims=True), own_score)
        weights = jnp.where(member, jnp.exp(scores - row_top), 0.0)
        own_weight = jnp.exp(own_score - row_top)
        row_total = jnp.sum(weights, axis=-1, keepdims=True) + own_weight
        summed = jnp.dot(
            weights.astype(jnp.bfloat16), vp_ref[:, cols], preferred_element_type=jnp.float32
        )
        own_bf = own_weight.astype(jnp.bfloat16).astype(jnp.float32)
        summed = summed + own_bf * vn_ref[:, cols].astype(jnp.float32)
        o_ref[:, cols] = (summed / row_total).astype(o_ref.dtype)


def attend_local(query_new, key_new, value_new, key_pool, value_pool, starts, ends, cos2, sin2):
    slots, width = query_new.shape
    rows = key_pool.shape[0]
    block = HEADS_PER_STEP * HD
    steps = width // block
    slot_spec = pl.BlockSpec((slots, block), lambda g: (0, g))
    pool_spec = pl.BlockSpec((rows, block), lambda g: (0, g))
    bound_spec = pl.BlockSpec((slots, 1), lambda g: (0, 0))
    table_spec = pl.BlockSpec((slots, HD), lambda g: (0, 0))
    flops = 4 * slots * rows * width
    return pl.pallas_call(
        attention_kernel,
        grid=(steps,),
        in_specs=[
            bound_spec,
            bound_spec,
            table_spec,
            table_spec,
            slot_spec,
            slot_spec,
            slot_spec,
            pool_spec,
            pool_spec,
        ],
        out_specs=slot_spec,
        out_shape=jax.ShapeDtypeStruct((slots, width), jnp.bfloat16),
        cost_estimate=pl.CostEstimate(
            flops=flops,
            transcendentals=slots * rows * (width // HD),
            bytes_accessed=2 * rows * width * 2 + 4 * slots * width * 2,
        ),
    )(starts, ends, cos2, sin2, query_new, key_new, value_new, key_pool, value_pool)


def gate_up_kernel(x_ref, w_ref, o_ref, acc, acc_sq):
    step = pl.program_id(0)
    quarters = x_ref.shape[1]
    width = x_ref.shape[3]
    columns = w_ref.shape[2]
    half = w_ref.shape[1] // 2
    units = o_ref.shape[0]

    @pl.when(step == 0)
    def _():
        acc[...] = jnp.zeros_like(acc)
        acc_sq[...] = jnp.zeros_like(acc_sq)

    def body(i, carry):
        weights = w_ref[i]
        for quarter in range(quarters):
            cols = slice(quarter * width, (quarter + 1) * width)
            block = x_ref[i, quarter, :columns, :]
            acc[:, cols] += jnp.dot(weights, block, preferred_element_type=jnp.float32)
            acc_sq[:, cols] += x_ref[i, quarter, columns:, :].astype(jnp.float32)
        return carry

    lax.fori_loop(0, x_ref.shape[0], body, 0)

    @pl.when(step == pl.num_programs(0) - 1)
    def _():
        squares = acc_sq[0:1, :] + acc_sq[1:2, :]
        inverse = lax.rsqrt(squares / D + 1e-05)
        gate_pre = acc[:half, :] * inverse
        silu = gate_pre / (1.0 + jnp.exp(-gate_pre))
        active = silu * (acc[half:, :] * inverse)
        o_ref[...] = active[:units].astype(o_ref.dtype)


def gate_up(hidden_t, weights_t, units):
    chunks, quarters, rows, width = hidden_t.shape
    both, columns = weights_t.shape[1], weights_t.shape[2]
    slots = quarters * width
    return pl.pallas_call(
        gate_up_kernel,
        grid=(chunks // R_PER_STEP,),
        in_specs=[
            pl.BlockSpec((R_PER_STEP, quarters, rows, width), lambda s: (s, 0, 0, 0)),
            pl.BlockSpec((R_PER_STEP, both, columns), lambda s: (s, 0, 0)),
        ],
        out_specs=pl.BlockSpec((units, slots), lambda s: (0, 0)),
        out_shape=jax.ShapeDtypeStruct((units, slots), jnp.bfloat16),
        scratch_shapes=[
            pltpu.VMEM((both, slots), jnp.float32),
            pltpu.VMEM((rows - columns, slots), jnp.float32),
        ],
        compiler_params=pltpu.CompilerParams(dimension_semantics=("arbitrary",)),
        cost_estimate=pl.CostEstimate(
            flops=2 * both * slots * chunks * columns,
            transcendentals=units * slots,
            bytes_accessed=hidden_t.size * 2 + weights_t.size * 2 + units * slots * 2,
        ),
    )(hidden_t, weights_t)


def body(
    query_new,
    key_new,
    value_new,
    key_pool,
    value_pool,
    lengths,
    slot_request,
    residual,
    out_proj,
    norm_gain,
    gate_proj,
    up_proj,
    down_proj,
):
    owned = query_new.shape[0]
    req_count = lax.axis_size(REQ)
    head_count = lax.axis_size(HEAD)
    first_slot = lax.axis_index(REQ) * owned
    my_requests = lax.dynamic_slice_in_dim(slot_request, first_slot, owned, 0)
    my_lengths = jnp.take(lengths, my_requests, axis=0)
    cosine, sine_table = rope_tables(my_lengths)
    cos2 = jnp.concatenate([cosine, cosine], axis=1)
    sin2 = jnp.concatenate([-sine_table, sine_table], axis=1)
    seg_ends = jnp.cumsum(my_lengths)
    starts = (seg_ends - my_lengths).astype(jnp.int32)
    attention = attend_local(
        query_new,
        key_new,
        value_new,
        key_pool,
        value_pool,
        starts[:, None],
        seg_ends.astype(jnp.int32)[:, None],
        cos2,
        sin2,
    )
    partial_sums = jnp.dot(
        lax.all_gather(attention, REQ, axis=0, tiled=True),
        out_proj,
        preferred_element_type=jnp.float32,
    )
    summed = lax.psum_scatter(partial_sums, HEAD, scatter_dimension=0, tiled=True)
    quarter = summed.shape[0]
    quarter_slots = lax.dynamic_slice_in_dim(
        slot_request, lax.axis_index(HEAD) * quarter, quarter, 0
    )
    attended = (jnp.take(residual, quarter_slots, axis=0).astype(jnp.float32) + summed).astype(
        jnp.bfloat16
    )
    column_width = attended.shape[1]
    widened = attended.astype(jnp.float32)
    partial_squares = jnp.sum(widened * widened, axis=1)
    high = partial_squares.astype(jnp.bfloat16)
    low = (partial_squares - high.astype(jnp.float32)).astype(jnp.bfloat16)
    pad_rows = SQ_ROWS - 2
    block_t = jnp.concatenate(
        [attended.T, high[None], low[None], jnp.zeros((pad_rows, quarter), jnp.bfloat16)], axis=0
    )
    hidden_t = lax.all_gather(block_t[None], REQ + (HEAD,), axis=0, tiled=True).reshape(
        req_count, head_count, column_width + SQ_ROWS, quarter
    )
    col_block = gate_proj.shape[1]
    gain = norm_gain.astype(jnp.float32)[:, None]
    padded = -(-col_block // 8) * 8

    def prepared(weights):
        scaled_w = (weights.astype(jnp.float32) * gain).astype(jnp.bfloat16)
        shaped_w = scaled_w.reshape(req_count, column_width, col_block).transpose(0, 2, 1)
        return jnp.pad(shaped_w, ((0, 0), (0, padded - col_block), (0, 0)))

    weights_t = jnp.concatenate([prepared(gate_proj), prepared(up_proj)], axis=1)
    active_t = gate_up(hidden_t, weights_t, col_block)
    active_all = lax.all_gather(active_t, HEAD, axis=0, tiled=True)
    cores = lax.axis_size(CORE)
    chips = req_count // cores
    units_all = active_all.shape[0]
    by_core = active_all.T.reshape(chips, cores, owned, units_all)
    my_core = lax.axis_index(CORE)

    def down_for(core):
        rows = lax.dynamic_index_in_dim(by_core, core, axis=1, keepdims=False)
        sums = jnp.dot(
            rows.reshape(chips * owned, units_all), down_proj, preferred_element_type=jnp.float32
        )
        return sums.astype(jnp.bfloat16).reshape(chips, owned, sums.shape[1])

    sent = down_for(cores - 1 - my_core)
    arrived = lax.ppermute(sent, CORE, [(core, cores - 1 - core) for core in range(cores)])
    kept = down_for(my_core)
    chip_sums = (kept.astype(jnp.float32) + arrived.astype(jnp.float32)).astype(jnp.bfloat16)
    received = lax.all_to_all(chip_sums, CHIPS, 0, 0, tiled=True)
    ffn_out = jnp.sum(received.astype(jnp.float32), axis=0).astype(jnp.bfloat16)
    return (attended, ffn_out)


def solution(mesh):
    placed = (
        P(REQ, HEAD),
        P(REQ, HEAD),
        P(REQ, HEAD),
        P(REQ, HEAD),
        P(REQ, HEAD),
        P(),
        P(),
        P(None, REQ),
        P(HEAD, REQ),
        P(),
        P(None, REQ + (HEAD,)),
        P(None, REQ + (HEAD,)),
        P(REQ, HEAD),
    )
    req_size, head_size = mesh.devices.shape
    named = jax.sharding.Mesh(
        mesh.devices.reshape(req_size // CORES_PER_CHIP, CORES_PER_CHIP, head_size),
        (CHIPS, CORE, HEAD),
    )
    return jax.shard_map(
        body,
        mesh=named,
        in_specs=placed,
        out_specs=(P(HEAD, REQ), P(REQ, HEAD)),
        check_vma=False,
    )
```
